256 devices in a mesh: seq: 32 (over z, y), dp: 8 (over x, core).
Axes of the slice: x: 4, y: 4, z: 8, core: 2. Of those that a mesh axis runs over, the one named last changes fastest.
Arguments:
- queries: bfloat16 [8, 12288, 2048], P('dp', 'seq'), may hold values from -0.59765625 to 0.59765625
- keys: bfloat16 [8, 12288, 2048], P('dp', 'seq'), may hold values from -0.59765625 to 0.59765625
- values: bfloat16 [8, 12288, 2048], P('dp', 'seq'), may hold values from -6 to 6
- output_gradient: bfloat16 [8, 12288, 2048], P('dp', 'seq'), may hold values from -0.59765625 to 0.59765625
- document_lengths: int32 [8, 8], P('dp'), may hold values from 1 to 3072, 12288 in all within a row
- cutoff_rows: int32 [8, 12288], P('dp', 'seq'), may hold values 0 or 1
- head_decay_rate: float32 [16], replicated, may hold values from 4.06901042e-06 to 0.04, as said below
Outputs:
- query_grad: bfloat16 [8, 12288, 2048], P('dp', 'seq')
- key_grad: bfloat16 [8, 12288, 2048], P('dp', 'seq')
- value_grad: bfloat16 [8, 12288, 2048], P('dp', 'seq')
- rate_grad: float32 [16], replicated
The draws below stay inside these ranges and needn't reach their ends.
Inputs may be any that keep to these rules, and one draw needn't show every extreme that they name: `head_decay_rate`: a positive rate for each head.
All inputs are finite; a program needn't handle non-finite values. No bound on the sum of `cutoff_rows` on one device may be relied on, other than what follows from the above.
Results may differ from the reference program's by a relative error of at most 0.0034.
Values sent between devices are 32-bit elements; how exact they have to be, the bound alone decides.
No kernel may reach another device: no remote copies, remote signals or barrier semaphores. Data moves between devices by JAX's collectives and lax.ppermute only.
A program may use at most 192 MiB of HBM per device.

```python
import math
import jax
import jax.numpy as jnp
import numpy as np
from jax import lax

HEADS = 16
HEAD_DIM = 128
BLOCK_TOKENS = 384
DOCS = 8
SEQUENCE_LENGTH = 12288
ALL_TOKENS = 98304
N_SEQ = 32
N_DP = 8


def draw_head_decay_rate(key, part):
    pick_key, slow_key, fast_key = jax.random.split(key, 3)
    slow_share = 0.5
    chosen = jax.random.uniform(pick_key, (HEADS,), jnp.float32) < slow_share
    slow_rate = jnp.exp(jnp.log(0.05 / SEQUENCE_LENGTH) + jax.random.uniform(slow_key, (HEADS,), jnp.float32) * jnp.log(10.0))
    fast_rate = jax.random.uniform(fast_key, (HEADS,), jnp.float32, minval=0.02, maxval=0.04)
    return jnp.where(chosen, slow_rate, fast_rate).astype(jnp.float32)


def with_ends(array, rng, smallest, largest):
    shape = array.shape
    index_at = [jax.random.randint(jax.random.fold_in(rng, axis), (), 0, shape[axis]) for axis in range(len(shape))]
    array = array.at[tuple(index_at)].set(smallest)
    longest = shape.index(max(shape))
    index_at[longest] = (index_at[longest] + 1) % shape[longest]
    return array.at[tuple(index_at)].set(largest)


def block_levels(rng, shape, cuts, smallest, top_value):
    gain, own = 1.0, jax.random.fold_in(rng, 6)
    for dim, blocks in cuts:
        heights = jnp.exp(jax.random.uniform(jax.random.fold_in(own, dim), (blocks,), jnp.float32, smallest / len(cuts), top_value / len(cuts)))
        gain = gain * jnp.repeat(heights, shape[dim] // blocks).reshape([-1 if axis == dim else 1 for axis in range(len(shape))])
    return gain


def length_profile(number_of, total, reach, skew):
    weights = [(1 << 20) // math.isqrt(grade ** skew) + 1 for grade in range(2, number_of + 1)]
    spare, counts = total - reach - (number_of - 1), [1] * (number_of - 1)
    while spare > 0:
        movable = [i for i in range(number_of - 1) if counts[i] < reach]
        mass, remaining = sum([weights[i] for i in movable]), spare
        for i in movable:
            extra = min(reach - counts[i], max(1, remaining * weights[i] // mass), spare)
            counts[i] = counts[i] + extra
            spare = spare - extra
    return np.array([reach] + counts)


def ragged_sizes(key, count, total, most, slope):
    if count == 2:
        one = jax.random.randint(key, (), max(1, total - most), min(most, total - 1) + 1)
        return jnp.stack([one, total - one])
    sizes = jnp.asarray(length_profile(count, total, most, slope), jnp.int32)
    couples = (count - 1) // 2
    source_of, receiver = sizes[1:1 + 2 * couples:2], sizes[2:2 + 2 * couples:2]
    slack = jnp.minimum(source_of - 1, most - receiver)
    passed = jax.random.randint(jax.random.fold_in(key, 1), (couples,), 0, 1 << 20) % (slack + 1)
    sizes = sizes.at[1:1 + 2 * couples:2].set(source_of - passed).at[2:2 + 2 * couples:2].set(receiver + passed)
    return sizes[jax.random.permutation(jax.random.fold_in(key, 2), count)]


def bell_draw(rng, shape, scale, bound, cuts=(), kind=jnp.bfloat16):
    result = jax.random.normal(rng, shape, jnp.float32) * scale
    if len(cuts) > 0:
        result = block_levels(rng, shape, cuts, -0.22, 0.18) * result
    return jnp.clip(result, min=-bound, max=bound).astype(kind)


def setup_inputs(seed: int = 0) -> dict:
    arg_keys = jax.random.split(jax.random.key(seed), 8)
    return {
        "queries": bell_draw(arg_keys[0], (N_DP, SEQUENCE_LENGTH, HEADS * HEAD_DIM), 0.1, 0.59765625, ((0, 8), (1, 32))),
        "keys": bell_draw(arg_keys[1], (N_DP, SEQUENCE_LENGTH, HEADS * HEAD_DIM), 0.1, 0.59765625, ((0, 8), (1, 32))),
        "values": bell_draw(arg_keys[2], (N_DP, SEQUENCE_LENGTH, HEADS * HEAD_DIM), 1.0, 6.0, ((0, 8), (1, 32))),
        "output_gradient": bell_draw(arg_keys[3], (N_DP, SEQUENCE_LENGTH, HEADS * HEAD_DIM), 0.1, 0.59765625, ((0, 8), (1, 32))),
        "document_lengths": jax.vmap(lambda own: ragged_sizes(own, DOCS, SEQUENCE_LENGTH, SEQUENCE_LENGTH // 4, 2))(jax.random.split(arg_keys[4], N_DP)).reshape((N_DP, DOCS)).astype(jnp.int32),
        "cutoff_rows": with_ends((jax.random.randint(arg_keys[5], (N_DP, SEQUENCE_LENGTH), 0, 8 * BLOCK_TOKENS) < 1).astype(jnp.int32), jax.random.fold_in(arg_keys[5], 1), 0, 1),
        "head_decay_rate": draw_head_decay_rate(jax.random.fold_in(arg_keys[7], 71), 0),
    }


cutoff_logarithm = math.log(0.7)
exact_mode = lax.Precision.HIGHEST

def block_mask_list(head_decay_rate, cutoff_list, row_position, start_list):
    is_start = jnp.any(row_position[:, None] == start_list[None, :], axis=1)
    seg_local = jnp.cumsum(is_start.astype(jnp.int32))
    begin = lax.optimization_barrier(jnp.max(jnp.where(start_list[None, :] <= row_position[:, None], start_list[None, :], 0), axis=1))
    position = (row_position - begin).astype(jnp.float32)
    logarithm_step = cutoff_list.astype(jnp.float32)[:, None] * cutoff_logarithm - head_decay_rate[None, :]
    cum_log = jnp.cumsum(logarithm_step, axis=0)
    carry_in = jnp.where((seg_local == 0)[:, None], jnp.exp(cum_log), 0.0)
    carry_out = jnp.where((seg_local == seg_local[-1])[:, None], jnp.exp(cum_log[-1][None, :] - cum_log), 0.0)
    decay_all = jnp.where(seg_local[-1] == 0, jnp.exp(cum_log[-1]), 0.0)
    return (cum_log, seg_local, position, carry_in, carry_out, decay_all)

def weights_of(cum_log, seg_local):
    count = seg_local.shape[0]
    index = jnp.arange(count, dtype=jnp.int32)
    allowed = (seg_local[:, None] == seg_local[None, :]) & (index[:, None] >= index[None, :])
    spread = cum_log.T[:, :, None] - cum_log.T[:, None, :]
    return jnp.where(allowed[None], jnp.exp(jnp.where(allowed[None], spread, 0.0)), 0.0)

def block_summary(query_block, key_block, value_block, gradient_block, carry_in, carry_out):
    scaled_keys = carry_out[:, :, None] * key_block.astype(jnp.float32)
    scaled_queries = carry_in[:, :, None] * query_block.astype(jnp.float32)
    state_local = jnp.einsum('the,thf->hef', scaled_keys, value_block.astype(jnp.float32), precision=exact_mode)
    back_local = jnp.einsum('she,shf->hef', scaled_queries, gradient_block.astype(jnp.float32), precision=exact_mode)
    return (state_local, back_local)

def block_finish(query_block, key_block, value_block, gradient_block, mask_list, state_input, backward_input):
    cum_log, seg_local, position, carry_in, carry_out, decay_all = mask_list
    query_f = query_block.astype(jnp.float32)
    key_f = key_block.astype(jnp.float32)
    value_f = value_block.astype(jnp.float32)
    grad_f = gradient_block.astype(jnp.float32)
    weight = weights_of(cum_log, seg_local)
    scores = jnp.einsum('she,the->hst', query_f, key_f, precision=exact_mode)
    grad_scores = jnp.einsum('shf,thf->hst', grad_f, value_f, precision=exact_mode)
    attn_prob = (weight * scores).astype(jnp.bfloat16).astype(jnp.float32)
    grad_prob = (weight * grad_scores).astype(jnp.bfloat16).astype(jnp.float32)
    value_full = jnp.einsum('hst,shf->thf', attn_prob, grad_f, precision=exact_mode)
    value_full = value_full + carry_out[:, :, None] * jnp.einsum('the,hef->thf', key_f, backward_input, precision=exact_mode)
    query_full = jnp.einsum('hst,the->she', grad_prob, key_f, precision=exact_mode)
    query_full = query_full + carry_in[:, :, None] * jnp.einsum('shf,hef->she', grad_f, state_input, precision=exact_mode)
    key_full = jnp.einsum('hst,she->the', grad_prob, query_f, precision=exact_mode)
    key_full = key_full + carry_out[:, :, None] * jnp.einsum('thf,hef->the', value_f, backward_input, precision=exact_mode)
    inner_step = lax.optimization_barrier(jnp.sum(key_f * key_full, axis=2)) - lax.optimization_barrier(jnp.sum(query_f * query_full, axis=2))
    rate_part = lax.optimization_barrier(jnp.sum(position[:, None] * inner_step, axis=0))
    return (query_full.astype(jnp.bfloat16), key_full.astype(jnp.bfloat16), value_full.astype(jnp.bfloat16), rate_part)

def reference(queries, keys, values, output_gradient, document_lengths, cutoff_rows, head_decay_rate):
    block_shape = (N_DP, N_SEQ, BLOCK_TOKENS, HEADS, HEAD_DIM)
    query_every = queries.reshape(block_shape)
    key_every = keys.reshape(block_shape)
    value_every = values.reshape(block_shape)
    gradient_every = output_gradient.reshape(block_shape)
    cutoff_every = cutoff_rows.reshape(N_DP, N_SEQ, BLOCK_TOKENS)
    block_number = jnp.arange(N_SEQ, dtype=jnp.int32)
    local_rows = jnp.arange(BLOCK_TOKENS, dtype=jnp.int32)

    def single_sequence(item_list):
        query_sequence, key_sequence, value_sequence, gradient_sequence, length_list, cutoff_list = item_list
        start_list = (jnp.cumsum(length_list) - length_list).astype(jnp.int32)

        def block_digest(inner_step):
            block_piece, query_block, key_block, value_block, gradient_block, cutoff_block = inner_step
            row_position = (block_piece * BLOCK_TOKENS + local_rows).astype(jnp.int32)
            mask_list = block_mask_list(head_decay_rate, cutoff_block, row_position, start_list)
            state_local, back_local = block_summary(query_block, key_block, value_block, gradient_block, mask_list[3], mask_list[4])
            return (mask_list[5], state_local, back_local)
        decay_list, state_list, backward_list = lax.map(block_digest, (block_number, query_sequence, key_sequence, value_sequence, gradient_sequence, cutoff_list))
        zero_state = jnp.zeros((HEADS, HEAD_DIM, HEAD_DIM), jnp.float32)

        def forward(carry, inner_step):
            decay, state = inner_step
            return (decay[:, None, None] * carry + state, carry)

        def backward(carry, inner_step):
            decay, back = inner_step
            return (back + decay[:, None, None] * carry, carry)
        unused_a, state_input = lax.scan(forward, zero_state, (decay_list, state_list))
        unused_b, backward_input = lax.scan(backward, zero_state, (decay_list, backward_list), reverse=True)

        def finish_step(inner_step):
            block_piece, query_block, key_block, value_block, gradient_block, cutoff_block, state_block, backward_block = inner_step
            row_position = (block_piece * BLOCK_TOKENS + local_rows).astype(jnp.int32)
            mask_list = block_mask_list(head_decay_rate, cutoff_block, row_position, start_list)
            return block_finish(query_block, key_block, value_block, gradient_block, mask_list, state_block, backward_block)
        return lax.map(finish_step, (block_number, query_sequence, key_sequence, value_sequence, gradient_sequence, cutoff_list, state_input, backward_input))
    query_output, key_output, value_output, rate_pieces = lax.map(single_sequence, (query_every, key_every, value_every, gradient_every, document_lengths, cutoff_every))
    full_shape = (N_DP, SEQUENCE_LENGTH, HEADS * HEAD_DIM)
    rate_total = lax.optimization_barrier(jnp.sum(rate_pieces, axis=(0, 1)))
    rate_grad = head_decay_rate * rate_total / math.sqrt(ALL_TOKENS)
    return (query_output.reshape(full_shape), key_output.reshape(full_shape), value_output.reshape(full_shape), rate_grad)
```

```python
import math

import jax
import jax.numpy as jnp
from jax import lax
from jax.sharding import PartitionSpec as P

HEADS = 16
HEAD_DIM = 128


cutoff_logarithm = math.log(0.7)
state_mode = lax.Precision.HIGH


def carried_both(decay, forward_part, backward_part, axis):
    count = lax.axis_size(axis)
    ones = jnp.ones_like(decay)
    zeros = jnp.zeros_like(forward_part)
    fwd_decay, fwd_state = decay, forward_part
    bwd_decay, bwd_state = decay, backward_part
    excl_decay, excl_state = ones, zeros
    rexcl_decay, rexcl_state = ones, zeros
    shift = 1
    while shift < count:
        up = [(i, i + shift) for i in range(count - shift)]
        down = [(i + shift, i) for i in range(count - shift)]
        got_decay, got_state = lax.ppermute((fwd_decay, fwd_state), axis, up)
        rgot_decay, rgot_state = lax.ppermute((bwd_decay, bwd_state), axis, down)
        excl_state = excl_decay[:, None, None] * got_state + excl_state
        excl_decay = got_decay * excl_decay
        rexcl_state = rexcl_state + rexcl_decay[:, None, None] * rgot_state
        rexcl_decay = rexcl_decay * rgot_decay
        if 2 * shift < count:
            fwd_state = fwd_decay[:, None, None] * got_state + fwd_state
            fwd_decay = got_decay * fwd_decay
            bwd_state = bwd_state + bwd_decay[:, None, None] * rgot_state
            bwd_decay = bwd_decay * rgot_decay
        shift *= 2
    return excl_state, rexcl_state


def block_mask_list(head_decay_rate, cutoff_list, row_position, start_list):
    is_start = jnp.any(row_position[:, None] == start_list[None, :], axis=1)
    seg_local = jnp.cumsum(is_start.astype(jnp.int32))
    begin = jnp.max(
        jnp.where(start_list[None, :] <= row_position[:, None], start_list[None, :], 0), axis=1
    )
    position = (row_position - begin).astype(jnp.float32)
    logarithm_step = (
        cutoff_list.astype(jnp.float32)[:, None] * cutoff_logarithm - head_decay_rate[None, :]
    )
    cum_log = jnp.cumsum(logarithm_step, axis=0)
    carry_in = jnp.where((seg_local == 0)[:, None], jnp.exp(cum_log), 0.0)
    carry_out = jnp.where(
        (seg_local == seg_local[-1])[:, None], jnp.exp(cum_log[-1][None, :] - cum_log), 0.0
    )
    decay_all = jnp.where(seg_local[-1] == 0, jnp.exp(cum_log[-1]), 0.0)
    return (cum_log, seg_local, position, carry_in, carry_out, decay_all)


def weights_of(cum_log, seg_local):
    count = seg_local.shape[0]
    index = jnp.arange(count, dtype=jnp.int32)
    allowed = (seg_local[:, None] == seg_local[None, :]) & (index[:, None] >= index[None, :])
    spread = cum_log.T[:, :, None] - cum_log.T[:, None, :]
    return jnp.where(allowed[None], jnp.exp(jnp.where(allowed[None], spread, 0.0)), 0.0)


def on_device(
    queries, keys, values, output_gradient, document_lengths, cutoff_rows, head_decay_rate
):
    row_count = queries.shape[1]
    query_block = queries.reshape(row_count, HEADS, HEAD_DIM)
    key_block = keys.reshape(row_count, HEADS, HEAD_DIM)
    value_block = values.reshape(row_count, HEADS, HEAD_DIM)
    gradient_block = output_gradient.reshape(row_count, HEADS, HEAD_DIM)
    block_piece = lax.axis_index("seq")
    row_position = block_piece * row_count + jnp.arange(row_count, dtype=jnp.int32)
    length_list = document_lengths[0]
    start_list = jnp.cumsum(length_list) - length_list
    cum_log, seg_local, position, carry_in, carry_out, decay_all = block_mask_list(
        head_decay_rate, cutoff_rows[0], row_position, start_list
    )
    key_f = key_block.astype(jnp.float32)
    value_f = value_block.astype(jnp.float32)
    grad_f = gradient_block.astype(jnp.float32)
    query_f = query_block.astype(jnp.float32)
    state_local = jnp.einsum(
        "the,thf->hef", carry_out[:, :, None] * key_f, value_f, precision=state_mode
    )
    back_local = jnp.einsum(
        "she,shf->hef", carry_in[:, :, None] * query_f, grad_f, precision=state_mode
    )
    state_input, backward_input = carried_both(decay_all, state_local, back_local, "seq")
    weight = weights_of(cum_log, seg_local)
    scores = jnp.einsum("she,the->hst", query_block, key_block, preferred_element_type=jnp.float32)
    grad_scores = jnp.einsum(
        "shf,thf->hst", gradient_block, value_block, preferred_element_type=jnp.float32
    )
    attn_prob = (weight * scores).astype(jnp.bfloat16)
    grad_prob = (weight * grad_scores).astype(jnp.bfloat16)
    value_full = jnp.einsum(
        "hst,shf->thf", attn_prob, gradient_block, preferred_element_type=jnp.float32
    )
    value_full = value_full + carry_out[:, :, None] * jnp.einsum(
        "the,hef->thf", key_f, backward_input, precision=state_mode
    )
    query_full = jnp.einsum(
        "hst,the->she", grad_prob, key_block, preferred_element_type=jnp.float32
    )
    query_full = query_full + carry_in[:, :, None] * jnp.einsum(
        "shf,hef->she", grad_f, state_input, precision=state_mode
    )
    key_full = jnp.einsum(
        "hst,she->the", grad_prob, query_block, preferred_element_type=jnp.float32
    )
    key_full = key_full + carry_out[:, :, None] * jnp.einsum(
        "thf,hef->the", value_f, backward_input, precision=state_mode
    )
    inner_step = jnp.sum(key_f * key_full, axis=2) - jnp.sum(query_f * query_full, axis=2)
    rate_part = jnp.sum(position[:, None] * inner_step, axis=0)
    rate_total = lax.psum(rate_part, ("seq", "dp"))
    token_total = row_count * lax.axis_size("seq") * lax.axis_size("dp")
    rate_grad = head_decay_rate * rate_total / math.sqrt(token_total)
    out_shape = (1, row_count, HEADS * HEAD_DIM)
    return (
        query_full.astype(jnp.bfloat16).reshape(out_shape),
        key_full.astype(jnp.bfloat16).reshape(out_shape),
        value_full.astype(jnp.bfloat16).reshape(out_shape),
        rate_grad,
    )


def solution(mesh):
    in_specs = (
        P("dp", "seq", None),
        P("dp", "seq", None),
        P("dp", "seq", None),
        P("dp", "seq", None),
        P("dp", None),
        P("dp", "seq"),
        P(),
    )
    out_specs = (P("dp", "seq", None), P("dp", "seq", None), P("dp", "seq", None), P())
    return jax.shard_map(
        on_device, mesh=mesh, in_specs=in_specs, out_specs=out_specs, check_vma=False
    )
```

```python
import math

import jax
import jax.numpy as jnp
from jax import lax
from jax.sharding import PartitionSpec as P

HEADS = 16
HEAD_DIM = 128


cutoff_logarithm = math.log(0.7)
state_mode = lax.Precision.HIGH


def packed(decay, state):
    pad = jnp.broadcast_to(decay[:, None, None], (state.shape[0], 8, state.shape[2]))
    return jnp.concatenate([state, pad], axis=1)


def combine(far, near):
    rows = far.shape[1] - 8
    state = near[:, rows : rows + 1, 0:1] * far[:, :rows] + near[:, :rows]
    return jnp.concatenate([state, far[:, rows:] * near[:, rows:]], axis=1)


def carried_both(decay, forward_part, backward_part, axis):
    count = lax.axis_size(axis)
    fwd = packed(decay, forward_part)
    bwd = packed(decay, backward_part)
    excl = packed(jnp.ones_like(decay), jnp.zeros_like(forward_part))
    rexcl = excl
    shift = 1
    while shift < count:
        up = [(i, i + shift) for i in range(count - shift)]
        down = [(i + shift, i) for i in range(count - shift)]
        got = lax.ppermute(fwd, axis, up)
        rgot = lax.ppermute(bwd, axis, down)
        excl = combine(got, excl)
        rexcl = combine(rgot, rexcl)
        if 2 * shift < count:
            fwd = combine(got, fwd)
            bwd = combine(rgot, bwd)
        shift *= 2
    rows = forward_part.shape[1]
    return excl[:, :rows], rexcl[:, :rows]


def all_sum(value, axes):
    for axis in axes:
        count = lax.axis_size(axis)
        step = 1
        while step < count:
            value = value + lax.ppermute(value, axis, [(i, i ^ step) for i in range(count)])
            step *= 2
    return value


def block_mask_list(head_decay_rate, cutoff_list, row_position, start_list):
    is_start = jnp.any(row_position[:, None] == start_list[None, :], axis=1)
    seg_local = jnp.cumsum(is_start.astype(jnp.int32))
    begin = jnp.max(
        jnp.where(start_list[None, :] <= row_position[:, None], start_list[None, :], 0), axis=1
    )
    position = (row_position - begin).astype(jnp.float32)
    logarithm_step = (
        cutoff_list.astype(jnp.float32)[:, None] * cutoff_logarithm - head_decay_rate[None, :]
    )
    cum_log = jnp.cumsum(logarithm_step, axis=0)
    carry_in = jnp.where((seg_local == 0)[:, None], jnp.exp(cum_log), 0.0)
    carry_out = jnp.where(
        (seg_local == seg_local[-1])[:, None], jnp.exp(cum_log[-1][None, :] - cum_log), 0.0
    )
    decay_all = jnp.where(seg_local[-1] == 0, jnp.exp(cum_log[-1]), 0.0)
    return (cum_log, seg_local, position, carry_in, carry_out, decay_all)


def weights_of(cum_log, seg_local):
    count = seg_local.shape[0]
    index = jnp.arange(count, dtype=jnp.int32)
    allowed = (seg_local[:, None] == seg_local[None, :]) & (index[:, None] >= index[None, :])
    spread = cum_log.T[:, :, None] - cum_log.T[:, None, :]
    return jnp.where(allowed[None], jnp.exp(jnp.where(allowed[None], spread, 0.0)), 0.0)


def on_device(
    queries, keys, values, output_gradient, document_lengths, cutoff_rows, head_decay_rate
):
    row_count = queries.shape[1]
    query_block = queries.reshape(row_count, HEADS, HEAD_DIM)
    key_block = keys.reshape(row_count, HEADS, HEAD_DIM)
    value_block = values.reshape(row_count, HEADS, HEAD_DIM)
    gradient_block = output_gradient.reshape(row_count, HEADS, HEAD_DIM)
    block_piece = lax.axis_index("seq")
    row_position = block_piece * row_count + jnp.arange(row_count, dtype=jnp.int32)
    length_list = document_lengths[0]
    start_list = jnp.cumsum(length_list) - length_list
    cum_log, seg_local, position, carry_in, carry_out, decay_all = block_mask_list(
        head_decay_rate, cutoff_rows[0], row_position, start_list
    )
    key_f = key_block.astype(jnp.float32)
    value_f = value_block.astype(jnp.float32)
    grad_f = gradient_block.astype(jnp.float32)
    query_f = query_block.astype(jnp.float32)
    state_local = jnp.einsum(
        "the,thf->hef", carry_out[:, :, None] * key_f, value_f, precision=state_mode
    )
    back_local = jnp.einsum(
        "she,shf->hef", carry_in[:, :, None] * query_f, grad_f, precision=state_mode
    )
    state_input, backward_input = carried_both(decay_all, state_local, back_local, "seq")
    weight = weights_of(cum_log, seg_local)
    scores = jnp.einsum("she,the->hst", query_block, key_block, preferred_element_type=jnp.float32)
    grad_scores = jnp.einsum(
        "shf,thf->hst", gradient_block, value_block, preferred_element_type=jnp.float32
    )
    attn_prob = (weight * scores).astype(jnp.bfloat16)
    grad_prob = (weight * grad_scores).astype(jnp.bfloat16)
    value_full = jnp.einsum(
        "hst,shf->thf", attn_prob, gradient_block, preferred_element_type=jnp.float32
    )
    value_full = value_full + carry_out[:, :, None] * jnp.einsum(
        "the,hef->thf", key_f, backward_input, precision=state_mode
    )
    query_full = jnp.einsum(
        "hst,the->she", grad_prob, key_block, preferred_element_type=jnp.float32
    )
    query_full = query_full + carry_in[:, :, None] * jnp.einsum(
        "shf,hef->she", grad_f, state_input, precision=state_mode
    )
    key_full = jnp.einsum(
        "hst,she->the", grad_prob, query_block, preferred_element_type=jnp.float32
    )
    key_full = key_full + carry_out[:, :, None] * jnp.einsum(
        "thf,hef->the", value_f, backward_input, precision=state_mode
    )
    inner_step = jnp.sum(key_f * key_full, axis=2) - jnp.sum(query_f * query_full, axis=2)
    rate_part = jnp.sum(position[:, None] * inner_step, axis=0)
    rate_total = all_sum(rate_part, ("seq", "dp"))
    token_total = row_count * lax.axis_size("seq") * lax.axis_size("dp")
    rate_grad = head_decay_rate * rate_total / math.sqrt(token_total)
    out_shape = (1, row_count, HEADS * HEAD_DIM)
    return (
        query_full.astype(jnp.bfloat16).reshape(out_shape),
        key_full.astype(jnp.bfloat16).reshape(out_shape),
        value_full.astype(jnp.bfloat16).reshape(out_shape),
        rate_grad,
    )


def solution(mesh):
    in_specs = (
        P("dp", "seq", None),
        P("dp", "seq", None),
        P("dp", "seq", None),
        P("dp", "seq", None),
        P("dp", None),
        P("dp", "seq"),
        P(),
    )
    out_specs = (P("dp", "seq", None), P("dp", "seq", None), P("dp", "seq", None), P())
    return jax.shard_map(
        on_device, mesh=mesh, in_specs=in_specs, out_specs=out_specs, check_vma=False
    )
```

```python
import math

import jax
import jax.numpy as jnp
from jax import lax
from jax.sharding import PartitionSpec as P

HEADS = 16
HEAD_DIM = 128


cutoff_logarithm = math.log(0.7)
state_mode = lax.Precision.HIGH


def packed(decay, state):
    pad = jnp.broadcast_to(decay[:, None, None], (state.shape[0], 8, state.shape[2]))
    return jnp.concatenate([state, pad], axis=1)


def combine(far, near):
    rows = far.shape[1] - 8
    state = near[:, rows : rows + 1, 0:1] * far[:, :rows] + near[:, :rows]
    return jnp.concatenate([state, far[:, rows:] * near[:, rows:]], axis=1)


def group_scan(fwd, bwd, axis, stride):
    count = lax.axis_size(axis)
    excl = jnp.concatenate([jnp.zeros_like(fwd[:, :-8]), jnp.ones_like(fwd[:, -8:])], axis=1)
    rexcl = excl
    shift = stride
    while shift < count:
        up = [(i, i + shift) for i in range(count - shift)]
        down = [(i + shift, i) for i in range(count - shift)]
        got = lax.ppermute(fwd, axis, up)
        rgot = lax.ppermute(bwd, axis, down)
        excl = combine(got, excl)
        rexcl = combine(rgot, rexcl)
        if 2 * shift < count:
            fwd = combine(got, fwd)
            bwd = combine(rgot, bwd)
        shift *= 2
    return excl, rexcl


def row_exchange(parts, axis, group):
    count = lax.axis_size(axis)
    place = lax.axis_index(axis) % group
    got = [lax.dynamic_index_in_dim(parts, place, 0, False)]
    for step in range(1, group):
        pairs = [
            (base + j, base + (j + step) % group)
            for base in range(0, count, group)
            for j in range(group)
        ]
        send = lax.dynamic_index_in_dim(parts, (place + step) % group, 0, False)
        got.append(lax.ppermute(send, axis, pairs))
    order = (place - jnp.arange(group)) % group
    return jnp.take(jnp.stack(got), order, axis=0)


def carried_both(decay, forward_part, backward_part, axis):
    count = lax.axis_size(axis)
    group = 4 if count % 4 == 0 and forward_part.shape[0] % 4 == 0 else 1
    heads, rows, cols = forward_part.shape
    share = heads // group
    pad = jnp.broadcast_to(decay[:, None, None], (heads, 8, cols))
    parts = jnp.concatenate([forward_part, backward_part, pad], axis=1)
    mine = row_exchange(parts.reshape(group, share, 2 * rows + 8, cols), axis, group)
    own_s = mine[:, :, :rows]
    own_b = mine[:, :, rows : 2 * rows]
    own_a = mine[:, :, 2 * rows, 0]
    excl = [jnp.zeros_like(own_s[0])]
    excl_a = [jnp.ones_like(own_a[0])]
    for j in range(1, group):
        excl.append(own_a[j - 1][:, None, None] * excl[j - 1] + own_s[j - 1])
        excl_a.append(excl_a[j - 1] * own_a[j - 1])
    total = own_a[group - 1][:, None, None] * excl[group - 1] + own_s[group - 1]
    total_a = excl_a[group - 1] * own_a[group - 1]
    later = [None] * group
    later_a = [None] * group
    later[group - 1] = jnp.zeros_like(own_b[0])
    later_a[group - 1] = jnp.ones_like(own_a[0])
    for j in range(group - 2, -1, -1):
        later[j] = own_b[j + 1] + own_a[j + 1][:, None, None] * later[j + 1]
        later_a[j] = own_a[j + 1] * later_a[j + 1]
    rtotal = own_b[0] + own_a[0][:, None, None] * later[0]
    before, after = group_scan(
        packed(total_a, total), packed(total_a, rtotal), axis, group
    )
    before = before[:, :rows]
    after = after[:, :rows]
    result = jnp.stack(
        [
            jnp.concatenate(
                [
                    excl_a[j][:, None, None] * before + excl[j],
                    later[j] + later_a[j][:, None, None] * after,
                ],
                axis=1,
            )
            for j in range(group)
        ]
    )
    full = row_exchange(result, axis, group).reshape(heads, 2 * rows, cols)
    return full[:, :rows], full[:, rows:]


def all_sum(value, axes):
    for axis in axes:
        count = lax.axis_size(axis)
        step = 1
        while step < count:
            value = value + lax.ppermute(value, axis, [(i, i ^ step) for i in range(count)])
            step *= 2
    return value


def block_mask_list(head_decay_rate, cutoff_list, row_position, start_list):
    is_start = jnp.any(row_position[:, None] == start_list[None, :], axis=1)
    seg_local = jnp.cumsum(is_start.astype(jnp.int32))
    begin = jnp.max(
        jnp.where(start_list[None, :] <= row_position[:, None], start_list[None, :], 0), axis=1
    )
    position = (row_position - begin).astype(jnp.float32)
    logarithm_step = (
        cutoff_list.astype(jnp.float32)[:, None] * cutoff_logarithm - head_decay_rate[None, :]
    )
    cum_log = jnp.cumsum(logarithm_step, axis=0)
    carry_in = jnp.where((seg_local == 0)[:, None], jnp.exp(cum_log), 0.0)
    carry_out = jnp.where(
        (seg_local == seg_local[-1])[:, None], jnp.exp(cum_log[-1][None, :] - cum_log), 0.0
    )
    decay_all = jnp.where(seg_local[-1] == 0, jnp.exp(cum_log[-1]), 0.0)
    return (cum_log, seg_local, position, carry_in, carry_out, decay_all)


def weights_of(cum_log, seg_local):
    count = seg_local.shape[0]
    index = jnp.arange(count, dtype=jnp.int32)
    allowed = (seg_local[:, None] == seg_local[None, :]) & (index[:, None] >= index[None, :])
    spread = cum_log.T[:, :, None] - cum_log.T[:, None, :]
    return jnp.where(allowed[None], jnp.exp(jnp.where(allowed[None], spread, 0.0)), 0.0)


def on_device(
    queries, keys, values, output_gradient, document_lengths, cutoff_rows, head_decay_rate
):
    row_count = queries.shape[1]
    query_block = queries.reshape(row_count, HEADS, HEAD_DIM)
    key_block = keys.reshape(row_count, HEADS, HEAD_DIM)
    value_block = values.reshape(row_count, HEADS, HEAD_DIM)
    gradient_block = output_gradient.reshape(row_count, HEADS, HEAD_DIM)
    block_piece = lax.axis_index("seq")
    row_position = block_piece * row_count + jnp.arange(row_count, dtype=jnp.int32)
    length_list = document_lengths[0]
    start_list = jnp.cumsum(length_list) - length_list
    cum_log, seg_local, position, carry_in, carry_out, decay_all = block_mask_list(
        head_decay_rate, cutoff_rows[0], row_position, start_list
    )
    key_f = key_block.astype(jnp.float32)
    value_f = value_block.astype(jnp.float32)
    grad_f = gradient_block.astype(jnp.float32)
    query_f = query_block.astype(jnp.float32)
    state_local = jnp.einsum(
        "the,thf->hef", carry_out[:, :, None] * key_f, value_f, precision=state_mode
    )
    back_local = jnp.einsum(
        "she,shf->hef", carry_in[:, :, None] * query_f, grad_f, precision=state_mode
    )
    state_input, backward_input = carried_both(decay_all, state_local, back_local, "seq")
    weight = weights_of(cum_log, seg_local)
    scores = jnp.einsum("she,the->hst", query_block, key_block, preferred_element_type=jnp.float32)
    grad_scores = jnp.einsum(
        "shf,thf->hst", gradient_block, value_block, preferred_element_type=jnp.float32
    )
    attn_prob = (weight * scores).astype(jnp.bfloat16)
    grad_prob = (weight * grad_scores).astype(jnp.bfloat16)
    value_full = jnp.einsum(
        "hst,shf->thf", attn_prob, gradient_block, preferred_element_type=jnp.float32
    )
    value_full = value_full + carry_out[:, :, None] * jnp.einsum(
        "the,hef->thf", key_f, backward_input, precision=state_mode
    )
    query_full = jnp.einsum(
        "hst,the->she", grad_prob, key_block, preferred_element_type=jnp.float32
    )
    query_full = query_full + carry_in[:, :, None] * jnp.einsum(
        "shf,hef->she", grad_f, state_input, precision=state_mode
    )
    key_full = jnp.einsum(
        "hst,she->the", grad_prob, query_block, preferred_element_type=jnp.float32
    )
    key_full = key_full + carry_out[:, :, None] * jnp.einsum(
        "thf,hef->the", value_f, backward_input, precision=state_mode
    )
    inner_step = jnp.sum(key_f * key_full, axis=2) - jnp.sum(query_f * query_full, axis=2)
    rate_part = jnp.sum(position[:, None] * inner_step, axis=0)
    rate_total = all_sum(rate_part, ("seq", "dp"))
    token_total = row_count * lax.axis_size("seq") * lax.axis_size("dp")
    rate_grad = head_decay_rate * rate_total / math.sqrt(token_total)
    out_shape = (1, row_count, HEADS * HEAD_DIM)
    return (
        query_full.astype(jnp.bfloat16).reshape(out_shape),
        key_full.astype(jnp.bfloat16).reshape(out_shape),
        value_full.astype(jnp.bfloat16).reshape(out_shape),
        rate_grad,
    )


def solution(mesh):
    in_specs = (
        P("dp", "seq", None),
        P("dp", "seq", None),
        P("dp", "seq", None),
        P("dp", "seq", None),
        P("dp", None),
        P("dp", "seq"),
        P(),
    )
    out_specs = (P("dp", "seq", None), P("dp", "seq", None), P("dp", "seq", None), P())
    return jax.shard_map(
        on_device, mesh=mesh, in_specs=in_specs, out_specs=out_specs, check_vma=False
    )
```

```python
import math

import jax
import jax.numpy as jnp
from jax import lax
from jax.sharding import PartitionSpec as P

HEADS = 16
HEAD_DIM = 128


cutoff_logarithm = math.log(0.7)
state_mode = lax.Precision.HIGH


def packed(decay, state):
    pad = jnp.broadcast_to(decay[:, None, None], (state.shape[0], 8, state.shape[2]))
    return jnp.concatenate([state, pad], axis=1)


def combine(far, near):
    rows = far.shape[1] - 8
    state = near[:, rows : rows + 1, 0:1] * far[:, :rows] + near[:, :rows]
    return jnp.concatenate([state, far[:, rows:] * near[:, rows:]], axis=1)


def group_scan(fwd, bwd, axis, stride):
    count = lax.axis_size(axis)
    excl = jnp.concatenate([jnp.zeros_like(fwd[:, :-8]), jnp.ones_like(fwd[:, -8:])], axis=1)
    rexcl = excl
    shift = stride
    while shift < count:
        up = [(i, i + shift) for i in range(count - shift)]
        down = [(i + shift, i) for i in range(count - shift)]
        got = lax.ppermute(fwd, axis, up)
        rgot = lax.ppermute(bwd, axis, down)
        excl = combine(got, excl)
        rexcl = combine(rgot, rexcl)
        if 2 * shift < count:
            fwd = combine(got, fwd)
            bwd = combine(rgot, bwd)
        shift *= 2
    return excl, rexcl


def row_exchange(parts, axis, group):
    count = lax.axis_size(axis)
    place = lax.axis_index(axis) % group
    got = [lax.dynamic_index_in_dim(parts, place, 0, False)]
    for step in range(1, group):
        pairs = [
            (base + j, base + (j + step) % group)
            for base in range(0, count, group)
            for j in range(group)
        ]
        send = lax.dynamic_index_in_dim(parts, (place + step) % group, 0, False)
        got.append(lax.ppermute(send, axis, pairs))
    order = (place - jnp.arange(group)) % group
    return jnp.take(jnp.stack(got), order, axis=0)


def carried_both(decay, forward_part, backward_part, axis):
    count = lax.axis_size(axis)
    group = 4 if count % 4 == 0 and forward_part.shape[0] % 4 == 0 else 1
    heads, rows, cols = forward_part.shape
    share = heads // group
    pad = jnp.broadcast_to(decay[:, None, None], (heads, 8, cols))
    parts = jnp.concatenate([forward_part, backward_part, pad], axis=1)
    mine = row_exchange(parts.reshape(group, share, 2 * rows + 8, cols), axis, group)
    own_s = mine[:, :, :rows]
    own_b = mine[:, :, rows : 2 * rows]
    own_a = mine[:, :, 2 * rows, 0]
    excl = [jnp.zeros_like(own_s[0])]
    excl_a = [jnp.ones_like(own_a[0])]
    for j in range(1, group):
        excl.append(own_a[j - 1][:, None, None] * excl[j - 1] + own_s[j - 1])
        excl_a.append(excl_a[j - 1] * own_a[j - 1])
    total = own_a[group - 1][:, None, None] * excl[group - 1] + own_s[group - 1]
    total_a = excl_a[group - 1] * own_a[group - 1]
    later = [None] * group
    later_a = [None] * group
    later[group - 1] = jnp.zeros_like(own_b[0])
    later_a[group - 1] = jnp.ones_like(own_a[0])
    for j in range(group - 2, -1, -1):
        later[j] = own_b[j + 1] + own_a[j + 1][:, None, None] * later[j + 1]
        later_a[j] = own_a[j + 1] * later_a[j + 1]
    rtotal = own_b[0] + own_a[0][:, None, None] * later[0]
    before, after = group_scan(
        packed(total_a, total), packed(total_a, rtotal), axis, group
    )
    before = before[:, :rows]
    after = after[:, :rows]
    result = jnp.stack(
        [
            jnp.concatenate(
                [
                    excl_a[j][:, None, None] * before + excl[j],
                    later[j] + later_a[j][:, None, None] * after,
                ],
                axis=1,
            )
            for j in range(group)
        ]
    )
    full = row_exchange(result, axis, group).reshape(heads, 2 * rows, cols)
    return full[:, :rows], full[:, rows:]


def all_sum(value, axes):
    for axis in axes:
        count = lax.axis_size(axis)
        step = 1
        while step < count:
            value = value + lax.ppermute(value, axis, [(i, i ^ step) for i in range(count)])
            step *= 2
    return value


def block_mask_list(head_decay_rate, cutoff_list, row_position, start_list):
    is_start = jnp.any(row_position[:, None] == start_list[None, :], axis=1)
    seg_local = jnp.cumsum(is_start.astype(jnp.int32))
    begin = jnp.max(
        jnp.where(start_list[None, :] <= row_position[:, None], start_list[None, :], 0), axis=1
    )
    position = (row_position - begin).astype(jnp.float32)
    logarithm_step = (
        cutoff_list.astype(jnp.float32)[:, None] * cutoff_logarithm - head_decay_rate[None, :]
    )
    cum_log = jnp.cumsum(logarithm_step, axis=0)
    carry_in = jnp.where((seg_local == 0)[:, None], jnp.exp(cum_log), 0.0)
    carry_out = jnp.where(
        (seg_local == seg_local[-1])[:, None], jnp.exp(cum_log[-1][None, :] - cum_log), 0.0
    )
    decay_all = jnp.where(seg_local[-1] == 0, jnp.exp(cum_log[-1]), 0.0)
    return (cum_log, seg_local, position, carry_in, carry_out, decay_all)


def weights_of(cum_log, seg_local):
    count = seg_local.shape[0]
    index = jnp.arange(count, dtype=jnp.int32)
    allowed = (seg_local[:, None] == seg_local[None, :]) & (index[:, None] >= index[None, :])
    spread = cum_log.T[:, :, None] - cum_log.T[:, None, :]
    return jnp.where(allowed[None], jnp.exp(jnp.where(allowed[None], spread, 0.0)), 0.0)


def on_device(
    queries, keys, values, output_gradient, document_lengths, cutoff_rows, head_decay_rate
):
    row_count = queries.shape[1]
    query_block = queries.reshape(row_count, HEADS, HEAD_DIM)
    key_block = keys.reshape(row_count, HEADS, HEAD_DIM)
    value_block = values.reshape(row_count, HEADS, HEAD_DIM)
    gradient_block = output_gradient.reshape(row_count, HEADS, HEAD_DIM)
    block_piece = lax.axis_index("seq")
    row_position = block_piece * row_count + jnp.arange(row_count, dtype=jnp.int32)
    length_list = document_lengths[0]
    start_list = jnp.cumsum(length_list) - length_list
    cum_log, seg_local, position, carry_in, carry_out, decay_all = block_mask_list(
        head_decay_rate, cutoff_rows[0], row_position, start_list
    )
    key_f = key_block.astype(jnp.float32)
    value_f = value_block.astype(jnp.float32)
    grad_f = gradient_block.astype(jnp.float32)
    query_f = query_block.astype(jnp.float32)
    state_local = jnp.einsum(
        "the,thf->hef", carry_out[:, :, None] * key_f, value_f, precision=state_mode
    )
    back_local = jnp.einsum(
        "she,shf->hef", carry_in[:, :, None] * query_f, grad_f, precision=state_mode
    )
    state_input, backward_input = carried_both(decay_all, state_local, back_local, "seq")
    weight = weights_of(cum_log, seg_local)
    scores = jnp.einsum("she,the->hst", query_block, key_block, preferred_element_type=jnp.float32)
    grad_scores = jnp.einsum(
        "shf,thf->hst", gradient_block, value_block, preferred_element_type=jnp.float32
    )
    attn_prob = (weight * scores).astype(jnp.bfloat16)
    grad_prob = (weight * grad_scores).astype(jnp.bfloat16)
    value_full = jnp.einsum(
        "hst,shf->thf", attn_prob, gradient_block, preferred_element_type=jnp.float32
    )
    value_full = value_full + carry_out[:, :, None] * jnp.einsum(
        "the,hef->thf", key_f, backward_input, precision=state_mode
    )
    query_local = jnp.einsum(
        "hst,the->she", grad_prob, key_block, preferred_element_type=jnp.float32
    )
    key_local = jnp.einsum(
        "hst,she->the", grad_prob, query_block, preferred_element_type=jnp.float32
    )
    local_step = jnp.sum(key_f * key_local, axis=2) - jnp.sum(query_f * query_local, axis=2)
    rate_local = jnp.sum(position[:, None] * local_step, axis=0)
    key_moment = jnp.einsum(
        "the,thf->hef",
        (position[:, None] * carry_out)[:, :, None] * key_f,
        value_f,
        precision=state_mode,
    )
    query_moment = jnp.einsum(
        "she,shf->hef",
        (position[:, None] * carry_in)[:, :, None] * query_f,
        grad_f,
        precision=state_mode,
    )
    rate_part = (
        rate_local
        + jnp.sum(key_moment * backward_input, axis=(1, 2))
        - jnp.sum(query_moment * state_input, axis=(1, 2))
    )
    query_full = query_local + carry_in[:, :, None] * jnp.einsum(
        "shf,hef->she", grad_f, state_input, precision=state_mode
    )
    key_full = key_local + carry_out[:, :, None] * jnp.einsum(
        "thf,hef->the", value_f, backward_input, precision=state_mode
    )
    rate_total = all_sum(rate_part, ("seq", "dp"))
    token_total = row_count * lax.axis_size("seq") * lax.axis_size("dp")
    rate_grad = head_decay_rate * rate_total / math.sqrt(token_total)
    out_shape = (1, row_count, HEADS * HEAD_DIM)
    return (
        query_full.astype(jnp.bfloat16).reshape(out_shape),
        key_full.astype(jnp.bfloat16).reshape(out_shape),
        value_full.astype(jnp.bfloat16).reshape(out_shape),
        rate_grad,
    )


def solution(mesh):
    in_specs = (
        P("dp", "seq", None),
        P("dp", "seq", None),
        P("dp", "seq", None),
        P("dp", "seq", None),
        P("dp", None),
        P("dp", "seq"),
        P(),
    )
    out_specs = (P("dp", "seq", None), P("dp", "seq", None), P("dp", "seq", None), P())
    return jax.shard_map(
        on_device, mesh=mesh, in_specs=in_specs, out_specs=out_specs, check_vma=False
    )
```

```python
import math

import jax
import jax.numpy as jnp
from jax import lax
from jax.sharding import PartitionSpec as P

HEADS = 16
HEAD_DIM = 128


cutoff_logarithm = math.log(0.7)
state_mode = lax.Precision.HIGH


def packed(decay, state):
    pad = jnp.broadcast_to(decay[:, None, None], (state.shape[0], 8, state.shape[2]))
    return jnp.concatenate([state, pad], axis=1)


def combine(far, near):
    rows = far.shape[1] - 8
    state = near[:, rows : rows + 1, 0:1] * far[:, :rows] + near[:, :rows]
    return jnp.concatenate([state, far[:, rows:] * near[:, rows:]], axis=1)


def group_scan(fwd, bwd, axis, stride):
    count = lax.axis_size(axis)
    excl = jnp.concatenate([jnp.zeros_like(fwd[:, :-8]), jnp.ones_like(fwd[:, -8:])], axis=1)
    rexcl = excl
    shift = stride
    while shift < count:
        up = [(i, i + shift) for i in range(count - shift)]
        down = [(i + shift, i) for i in range(count - shift)]
        got = lax.ppermute(fwd, axis, up)
        rgot = lax.ppermute(bwd, axis, down)
        excl = combine(got, excl)
        rexcl = combine(rgot, rexcl)
        if 2 * shift < count:
            fwd = combine(got, fwd)
            bwd = combine(rgot, bwd)
        shift *= 2
    return excl, rexcl


def row_exchange(parts, axis, group):
    count = lax.axis_size(axis)
    place = lax.axis_index(axis) % group
    got = [lax.dynamic_index_in_dim(parts, place, 0, False)]
    for step in range(1, group):
        pairs = [
            (base + j, base + (j + step) % group)
            for base in range(0, count, group)
            for j in range(group)
        ]
        send = lax.dynamic_index_in_dim(parts, (place + step) % group, 0, False)
        got.append(lax.ppermute(send, axis, pairs))
    return jnp.stack([lax.select_n((place - j) % group, *got) for j in range(group)])


def carried_both(decay, forward_part, backward_part, axis):
    count = lax.axis_size(axis)
    group = 4 if count % 4 == 0 and forward_part.shape[0] % 4 == 0 else 1
    heads, rows, cols = forward_part.shape
    share = heads // group
    pad = jnp.broadcast_to(decay[:, None, None], (heads, 8, cols))
    parts = jnp.concatenate([forward_part, backward_part, pad], axis=1)
    mine = row_exchange(parts.reshape(group, share, 2 * rows + 8, cols), axis, group)
    own_s = mine[:, :, :rows]
    own_b = mine[:, :, rows : 2 * rows]
    own_a = mine[:, :, 2 * rows, 0]
    excl = [jnp.zeros_like(own_s[0])]
    excl_a = [jnp.ones_like(own_a[0])]
    for j in range(1, group):
        excl.append(own_a[j - 1][:, None, None] * excl[j - 1] + own_s[j - 1])
        excl_a.append(excl_a[j - 1] * own_a[j - 1])
    total = own_a[group - 1][:, None, None] * excl[group - 1] + own_s[group - 1]
    total_a = excl_a[group - 1] * own_a[group - 1]
    later = [None] * group
    later_a = [None] * group
    later[group - 1] = jnp.zeros_like(own_b[0])
    later_a[group - 1] = jnp.ones_like(own_a[0])
    for j in range(group - 2, -1, -1):
        later[j] = own_b[j + 1] + own_a[j + 1][:, None, None] * later[j + 1]
        later_a[j] = own_a[j + 1] * later_a[j + 1]
    rtotal = own_b[0] + own_a[0][:, None, None] * later[0]
    before, after = group_scan(
        packed(total_a, total), packed(total_a, rtotal), axis, group
    )
    before = before[:, :rows]
    after = after[:, :rows]
    result = jnp.stack(
        [
            jnp.concatenate(
                [
                    excl_a[j][:, None, None] * before + excl[j],
                    later[j] + later_a[j][:, None, None] * after,
                ],
                axis=1,
            )
            for j in range(group)
        ]
    )
    full = row_exchange(result, axis, group).reshape(heads, 2 * rows, cols)
    return full[:, :rows], full[:, rows:]


def digit_sum(value, axis, step, radix):
    count = lax.axis_size(axis)
    digit = (lax.axis_index(axis) // step) % radix
    got = [value]
    for k in range(1, radix):
        got.append(lax.ppermute(value, axis, [(i, i ^ (k * step)) for i in range(count)]))
    total = lax.select_n(digit, *got)
    for m in range(1, radix):
        total = total + lax.select_n(digit ^ m, *got)
    return total


def all_sum(value, axes):
    for axis in axes:
        count = lax.axis_size(axis)
        step = 1
        while step < count:
            radix = 4 if count % (step * 4) == 0 else 2
            value = digit_sum(value, axis, step, radix)
            step *= radix
    return value


def block_mask_list(head_decay_rate, cutoff_list, row_position, start_list):
    is_start = jnp.any(row_position[:, None] == start_list[None, :], axis=1)
    seg_local = jnp.cumsum(is_start.astype(jnp.int32))
    begin = jnp.max(
        jnp.where(start_list[None, :] <= row_position[:, None], start_list[None, :], 0), axis=1
    )
    position = (row_position - begin).astype(jnp.float32)
    logarithm_step = (
        cutoff_list.astype(jnp.float32)[:, None] * cutoff_logarithm - head_decay_rate[None, :]
    )
    cum_log = jnp.cumsum(logarithm_step, axis=0)
    carry_in = jnp.where((seg_local == 0)[:, None], jnp.exp(cum_log), 0.0)
    carry_out = jnp.where(
        (seg_local == seg_local[-1])[:, None], jnp.exp(cum_log[-1][None, :] - cum_log), 0.0
    )
    decay_all = jnp.where(seg_local[-1] == 0, jnp.exp(cum_log[-1]), 0.0)
    return (cum_log, seg_local, position, carry_in, carry_out, decay_all)


def weights_of(cum_log, seg_local):
    count = seg_local.shape[0]
    index = jnp.arange(count, dtype=jnp.int32)
    allowed = (seg_local[:, None] == seg_local[None, :]) & (index[:, None] >= index[None, :])
    spread = cum_log.T[:, :, None] - cum_log.T[:, None, :]
    return jnp.where(allowed[None], jnp.exp(jnp.where(allowed[None], spread, 0.0)), 0.0)


def on_device(
    queries, keys, values, output_gradient, document_lengths, cutoff_rows, head_decay_rate
):
    row_count = queries.shape[1]
    query_block = queries.reshape(row_count, HEADS, HEAD_DIM)
    key_block = keys.reshape(row_count, HEADS, HEAD_DIM)
    value_block = values.reshape(row_count, HEADS, HEAD_DIM)
    gradient_block = output_gradient.reshape(row_count, HEADS, HEAD_DIM)
    block_piece = lax.axis_index("seq")
    row_position = block_piece * row_count + jnp.arange(row_count, dtype=jnp.int32)
    length_list = document_lengths[0]
    start_list = jnp.cumsum(length_list) - length_list
    cum_log, seg_local, position, carry_in, carry_out, decay_all = block_mask_list(
        head_decay_rate, cutoff_rows[0], row_position, start_list
    )
    key_f = key_block.astype(jnp.float32)
    value_f = value_block.astype(jnp.float32)
    grad_f = gradient_block.astype(jnp.float32)
    query_f = query_block.astype(jnp.float32)
    state_local = jnp.einsum(
        "the,thf->hef", carry_out[:, :, None] * key_f, value_f, precision=state_mode
    )
    back_local = jnp.einsum(
        "she,shf->hef", carry_in[:, :, None] * query_f, grad_f, precision=state_mode
    )
    state_input, backward_input = carried_both(decay_all, state_local, back_local, "seq")
    weight = weights_of(cum_log, seg_local)
    scores = jnp.einsum("she,the->hst", query_block, key_block, preferred_element_type=jnp.float32)
    grad_scores = jnp.einsum(
        "shf,thf->hst", gradient_block, value_block, preferred_element_type=jnp.float32
    )
    attn_prob = (weight * scores).astype(jnp.bfloat16)
    grad_prob = (weight * grad_scores).astype(jnp.bfloat16)
    value_full = jnp.einsum(
        "hst,shf->thf", attn_prob, gradient_block, preferred_element_type=jnp.float32
    )
    value_full = value_full + carry_out[:, :, None] * jnp.einsum(
        "the,hef->thf", key_f, backward_input, precision=state_mode
    )
    query_full = jnp.einsum(
        "hst,the->she", grad_prob, key_block, preferred_element_type=jnp.float32
    )
    query_full = query_full + carry_in[:, :, None] * jnp.einsum(
        "shf,hef->she", grad_f, state_input, precision=state_mode
    )
    key_full = jnp.einsum(
        "hst,she->the", grad_prob, query_block, preferred_element_type=jnp.float32
    )
    key_full = key_full + carry_out[:, :, None] * jnp.einsum(
        "thf,hef->the", value_f, backward_input, precision=state_mode
    )
    inner_step = jnp.sum(key_f * key_full, axis=2) - jnp.sum(query_f * query_full, axis=2)
    rate_part = jnp.sum(position[:, None] * inner_step, axis=0)
    rate_total = all_sum(rate_part, ("seq", "dp"))
    token_total = row_count * lax.axis_size("seq") * lax.axis_size("dp")
    rate_grad = head_decay_rate * rate_total / math.sqrt(token_total)
    out_shape = (1, row_count, HEADS * HEAD_DIM)
    return (
        query_full.astype(jnp.bfloat16).reshape(out_shape),
        key_full.astype(jnp.bfloat16).reshape(out_shape),
        value_full.astype(jnp.bfloat16).reshape(out_shape),
        rate_grad,
    )


def solution(mesh):
    in_specs = (
        P("dp", "seq", None),
        P("dp", "seq", None),
        P("dp", "seq", None),
        P("dp", "seq", None),
        P("dp", None),
        P("dp", "seq"),
        P(),
    )
    out_specs = (P("dp", "seq", None), P("dp", "seq", None), P("dp", "seq", None), P())
    return jax.shard_map(
        on_device, mesh=mesh, in_specs=in_specs, out_specs=out_specs, check_vma=False
    )
```

```python
import math

import jax
import jax.numpy as jnp
from jax import lax
from jax.sharding import PartitionSpec as P
from jax.experimental import pallas as pl

HEADS = 16
HEAD_DIM = 128


cutoff_logarithm = math.log(0.7)
state_mode = lax.Precision.HIGH


def packed(decay, state):
    pad = jnp.broadcast_to(decay[:, None, None], (state.shape[0], 8, state.shape[2]))
    return jnp.concatenate([state, pad], axis=1)


def combine(far, near):
    rows = far.shape[1] - 8
    state = near[:, rows : rows + 1, 0:1] * far[:, :rows] + near[:, :rows]
    return jnp.concatenate([state, far[:, rows:] * near[:, rows:]], axis=1)


def group_scan(fwd, bwd, axis, stride):
    count = lax.axis_size(axis)
    excl = jnp.concatenate([jnp.zeros_like(fwd[:, :-8]), jnp.ones_like(fwd[:, -8:])], axis=1)
    rexcl = excl
    shift = stride
    while shift < count:
        up = [(i, i + shift) for i in range(count - shift)]
        down = [(i + shift, i) for i in range(count - shift)]
        if 2 * shift >= count:
            place = lax.axis_index(axis)
            sent = jnp.where(place < count - shift, fwd, bwd)
            got = lax.ppermute(sent, axis, up + down)
            excl = jnp.where(place >= shift, combine(got, excl), excl)
            rexcl = jnp.where(place < count - shift, combine(got, rexcl), rexcl)
            break
        got = lax.ppermute(fwd, axis, up)
        rgot = lax.ppermute(bwd, axis, down)
        excl = combine(got, excl)
        rexcl = combine(rgot, rexcl)
        if 2 * shift < count:
            fwd = combine(got, fwd)
            bwd = combine(rgot, bwd)
        shift *= 2
    return excl, rexcl


def row_exchange(parts, axis, group):
    count = lax.axis_size(axis)
    place = lax.axis_index(axis) % group
    got = [lax.dynamic_index_in_dim(parts, place, 0, False)]
    for step in range(1, group):
        pairs = [
            (base + j, base + (j + step) % group)
            for base in range(0, count, group)
            for j in range(group)
        ]
        send = lax.dynamic_index_in_dim(parts, (place + step) % group, 0, False)
        got.append(lax.ppermute(send, axis, pairs))
    return jnp.stack([lax.select_n((place - j) % group, *got) for j in range(group)])


def carried_both(decay, forward_part, backward_part, axis):
    count = lax.axis_size(axis)
    group = 4 if count % 4 == 0 and forward_part.shape[0] % 4 == 0 else 1
    heads, rows, cols = forward_part.shape
    share = heads // group
    pad = jnp.broadcast_to(decay[:, None, None], (heads, 8, cols))
    parts = jnp.concatenate([forward_part, backward_part, pad], axis=1)
    mine = row_exchange(parts.reshape(group, share, 2 * rows + 8, cols), axis, group)
    own_s = mine[:, :, :rows]
    own_b = mine[:, :, rows : 2 * rows]
    own_a = mine[:, :, 2 * rows, 0]
    excl = [jnp.zeros_like(own_s[0])]
    excl_a = [jnp.ones_like(own_a[0])]
    for j in range(1, group):
        excl.append(own_a[j - 1][:, None, None] * excl[j - 1] + own_s[j - 1])
        excl_a.append(excl_a[j - 1] * own_a[j - 1])
    total = own_a[group - 1][:, None, None] * excl[group - 1] + own_s[group - 1]
    total_a = excl_a[group - 1] * own_a[group - 1]
    later = [None] * group
    later_a = [None] * group
    later[group - 1] = jnp.zeros_like(own_b[0])
    later_a[group - 1] = jnp.ones_like(own_a[0])
    for j in range(group - 2, -1, -1):
        later[j] = own_b[j + 1] + own_a[j + 1][:, None, None] * later[j + 1]
        later_a[j] = own_a[j + 1] * later_a[j + 1]
    rtotal = own_b[0] + own_a[0][:, None, None] * later[0]
    before, after = group_scan(
        packed(total_a, total), packed(total_a, rtotal), axis, group
    )
    before = before[:, :rows]
    after = after[:, :rows]
    result = jnp.stack(
        [
            jnp.concatenate(
                [
                    excl_a[j][:, None, None] * before + excl[j],
                    later[j] + later_a[j][:, None, None] * after,
                ],
                axis=1,
            )
            for j in range(group)
        ]
    )
    full = row_exchange(result, axis, group).reshape(heads, 2 * rows, cols)
    return full[:, :rows], full[:, rows:]


def digit_sum(value, axis, step, radix):
    count = lax.axis_size(axis)
    digit = (lax.axis_index(axis) // step) % radix
    got = [value]
    for k in range(1, radix):
        got.append(lax.ppermute(value, axis, [(i, i ^ (k * step)) for i in range(count)]))
    total = lax.select_n(digit, *got)
    for m in range(1, radix):
        total = total + lax.select_n(digit ^ m, *got)
    return total


def all_sum(value, axes):
    for axis in axes:
        count = lax.axis_size(axis)
        step = 1
        while step < count:
            radix = 4 if count % (step * 4) == 0 else 2
            value = digit_sum(value, axis, step, radix)
            step *= radix
    return value


def split_dot(scaled, other):
    high = scaled.astype(jnp.bfloat16)
    low = (scaled - high.astype(jnp.float32)).astype(jnp.bfloat16)
    return jnp.dot(high, other, preferred_element_type=jnp.float32) + jnp.dot(
        low, other, preferred_element_type=jnp.float32
    )


def summary_kernel(out_ref, in_ref, key_ref, value_ref, query_ref, grad_ref, state_ref, back_ref):
    per = state_ref.shape[0]
    width = state_ref.shape[2]
    for j in range(per):
        cols = slice(j * width, (j + 1) * width)
        keys_t = (out_ref[j] * key_ref[0, :, cols].astype(jnp.float32)).T
        state_ref[j] = split_dot(keys_t, value_ref[0, :, cols])
        query_t = (in_ref[j] * query_ref[0, :, cols].astype(jnp.float32)).T
        back_ref[j] = split_dot(query_t, grad_ref[0, :, cols])


def block_summaries(carry_out, carry_in, keys, values, queries, output_gradient):
    rows = keys.shape[1]
    per = 4
    steps = HEADS // per
    carry_spec = pl.BlockSpec((per, rows, 1), lambda i: (i, 0, 0))
    data_spec = pl.BlockSpec((1, rows, per * HEAD_DIM), lambda i: (0, 0, i))
    out_spec = pl.BlockSpec((per, HEAD_DIM, HEAD_DIM), lambda i: (i, 0, 0))
    shape = jax.ShapeDtypeStruct((HEADS, HEAD_DIM, HEAD_DIM), jnp.float32)
    return pl.pallas_call(
        summary_kernel,
        grid=(steps,),
        in_specs=[carry_spec, carry_spec, data_spec, data_spec, data_spec, data_spec],
        out_specs=[out_spec, out_spec],
        out_shape=[shape, shape],
    )(carry_out.T[:, :, None], carry_in.T[:, :, None], keys, values, queries, output_gradient)


def block_mask_list(head_decay_rate, cutoff_list, row_position, start_list):
    is_start = jnp.any(row_position[:, None] == start_list[None, :], axis=1)
    seg_local = jnp.cumsum(is_start.astype(jnp.int32))
    begin = jnp.max(
        jnp.where(start_list[None, :] <= row_position[:, None], start_list[None, :], 0), axis=1
    )
    position = (row_position - begin).astype(jnp.float32)
    logarithm_step = (
        cutoff_list.astype(jnp.float32)[:, None] * cutoff_logarithm - head_decay_rate[None, :]
    )
    cum_log = jnp.cumsum(logarithm_step, axis=0)
    carry_in = jnp.where((seg_local == 0)[:, None], jnp.exp(cum_log), 0.0)
    carry_out = jnp.where(
        (seg_local == seg_local[-1])[:, None], jnp.exp(cum_log[-1][None, :] - cum_log), 0.0
    )
    decay_all = jnp.where(seg_local[-1] == 0, jnp.exp(cum_log[-1]), 0.0)
    return (cum_log, seg_local, position, carry_in, carry_out, decay_all)


def weights_of(cum_log, seg_local):
    count = seg_local.shape[0]
    index = jnp.arange(count, dtype=jnp.int32)
    allowed = (seg_local[:, None] == seg_local[None, :]) & (index[:, None] >= index[None, :])
    spread = cum_log.T[:, :, None] - cum_log.T[:, None, :]
    return jnp.where(allowed[None], jnp.exp(jnp.where(allowed[None], spread, 0.0)), 0.0)


def on_device(
    queries, keys, values, output_gradient, document_lengths, cutoff_rows, head_decay_rate
):
    row_count = queries.shape[1]
    query_block = queries.reshape(row_count, HEADS, HEAD_DIM)
    key_block = keys.reshape(row_count, HEADS, HEAD_DIM)
    value_block = values.reshape(row_count, HEADS, HEAD_DIM)
    gradient_block = output_gradient.reshape(row_count, HEADS, HEAD_DIM)
    block_piece = lax.axis_index("seq")
    row_position = block_piece * row_count + jnp.arange(row_count, dtype=jnp.int32)
    length_list = document_lengths[0]
    start_list = jnp.cumsum(length_list) - length_list
    cum_log, seg_local, position, carry_in, carry_out, decay_all = block_mask_list(
        head_decay_rate, cutoff_rows[0], row_position, start_list
    )
    key_f = key_block.astype(jnp.float32)
    value_f = value_block.astype(jnp.float32)
    grad_f = gradient_block.astype(jnp.float32)
    query_f = query_block.astype(jnp.float32)
    state_local, back_local = block_summaries(
        carry_out, carry_in, keys, values, queries, output_gradient
    )
    state_input, backward_input = carried_both(decay_all, state_local, back_local, "seq")
    weight = weights_of(cum_log, seg_local)
    scores = jnp.einsum("she,the->hst", query_block, key_block, preferred_element_type=jnp.float32)
    grad_scores = jnp.einsum(
        "shf,thf->hst", gradient_block, value_block, preferred_element_type=jnp.float32
    )
    attn_prob = (weight * scores).astype(jnp.bfloat16)
    grad_prob = (weight * grad_scores).astype(jnp.bfloat16)
    value_full = jnp.einsum(
        "hst,shf->thf", attn_prob, gradient_block, preferred_element_type=jnp.float32
    )
    value_full = value_full + carry_out[:, :, None] * jnp.einsum(
        "the,hef->thf", key_f, backward_input, precision=state_mode
    )
    query_full = jnp.einsum(
        "hst,the->she", grad_prob, key_block, preferred_element_type=jnp.float32
    )
    query_full = query_full + carry_in[:, :, None] * jnp.einsum(
        "shf,hef->she", grad_f, state_input, precision=state_mode
    )
    key_full = jnp.einsum(
        "hst,she->the", grad_prob, query_block, preferred_element_type=jnp.float32
    )
    key_full = key_full + carry_out[:, :, None] * jnp.einsum(
        "thf,hef->the", value_f, backward_input, precision=state_mode
    )
    inner_step = jnp.sum(key_f * key_full, axis=2) - jnp.sum(query_f * query_full, axis=2)
    rate_part = jnp.sum(position[:, None] * inner_step, axis=0)
    rate_total = all_sum(rate_part, ("seq", "dp"))
    token_total = row_count * lax.axis_size("seq") * lax.axis_size("dp")
    rate_grad = head_decay_rate * rate_total / math.sqrt(token_total)
    out_shape = (1, row_count, HEADS * HEAD_DIM)
    return (
        query_full.astype(jnp.bfloat16).reshape(out_shape),
        key_full.astype(jnp.bfloat16).reshape(out_shape),
        value_full.astype(jnp.bfloat16).reshape(out_shape),
        rate_grad,
    )


def solution(mesh):
    in_specs = (
        P("dp", "seq", None),
        P("dp", "seq", None),
        P("dp", "seq", None),
        P("dp", "seq", None),
        P("dp", None),
        P("dp", "seq"),
        P(),
    )
    out_specs = (P("dp", "seq", None), P("dp", "seq", None), P("dp", "seq", None), P())
    return jax.shard_map(
        on_device, mesh=mesh, in_specs=in_specs, out_specs=out_specs, check_vma=False
    )
```

```python
import math

import jax
import jax.numpy as jnp
from jax import lax
from jax.sharding import PartitionSpec as P

HEADS = 16
HEAD_DIM = 128


cutoff_logarithm = math.log(0.7)
state_mode = lax.Precision.HIGH


def packed(decay, state):
    pad = jnp.broadcast_to(decay[:, None, None], (state.shape[0], 8, state.shape[2]))
    return jnp.concatenate([state, pad], axis=1)


def combine(far, near):
    rows = far.shape[1] - 8
    state = near[:, rows : rows + 1, 0:1] * far[:, :rows] + near[:, :rows]
    return jnp.concatenate([state, far[:, rows:] * near[:, rows:]], axis=1)


def group_scan(fwd, bwd, axis, stride):
    count = lax.axis_size(axis)
    excl = jnp.concatenate([jnp.zeros_like(fwd[:, :-8]), jnp.ones_like(fwd[:, -8:])], axis=1)
    rexcl = excl
    shift = stride
    while shift < count:
        up = [(i, i + shift) for i in range(count - shift)]
        down = [(i + shift, i) for i in range(count - shift)]
        if 2 * shift >= count:
            place = lax.axis_index(axis)
            sent = jnp.where(place < count - shift, fwd, bwd)
            got = lax.ppermute(sent, axis, up + down)
            excl = jnp.where(place >= shift, combine(got, excl), excl)
            rexcl = jnp.where(place < count - shift, combine(got, rexcl), rexcl)
            break
        got = lax.ppermute(fwd, axis, up)
        rgot = lax.ppermute(bwd, axis, down)
        excl = combine(got, excl)
        rexcl = combine(rgot, rexcl)
        if 2 * shift < count:
            fwd = combine(got, fwd)
            bwd = combine(rgot, bwd)
        shift *= 2
    return excl, rexcl


def row_exchange(parts, axis, group):
    count = lax.axis_size(axis)
    place = lax.axis_index(axis) % group
    got = [lax.dynamic_index_in_dim(parts, place, 0, False)]
    for step in range(1, group):
        pairs = [
            (base + j, base + (j + step) % group)
            for base in range(0, count, group)
            for j in range(group)
        ]
        send = lax.dynamic_index_in_dim(parts, (place + step) % group, 0, False)
        got.append(lax.ppermute(send, axis, pairs))
    return jnp.stack([lax.select_n((place - j) % group, *got) for j in range(group)])


def carried_both(decay, forward_part, backward_part, axis, extra):
    count = lax.axis_size(axis)
    group = 4 if count % 4 == 0 and forward_part.shape[0] % 4 == 0 else 1
    heads, rows, cols = forward_part.shape
    share = heads // group
    pad = jnp.broadcast_to(decay[:, None, None], (heads, 8, cols))
    parts = jnp.concatenate([forward_part, backward_part, pad], axis=1)
    mine = row_exchange(parts.reshape(group, share, 2 * rows + 8, cols), axis, group)
    mine, extra = lax.optimization_barrier((mine, extra))
    own_s = mine[:, :, :rows]
    own_b = mine[:, :, rows : 2 * rows]
    own_a = mine[:, :, 2 * rows, 0]
    excl = [jnp.zeros_like(own_s[0])]
    excl_a = [jnp.ones_like(own_a[0])]
    for j in range(1, group):
        excl.append(own_a[j - 1][:, None, None] * excl[j - 1] + own_s[j - 1])
        excl_a.append(excl_a[j - 1] * own_a[j - 1])
    total = own_a[group - 1][:, None, None] * excl[group - 1] + own_s[group - 1]
    total_a = excl_a[group - 1] * own_a[group - 1]
    later = [None] * group
    later_a = [None] * group
    later[group - 1] = jnp.zeros_like(own_b[0])
    later_a[group - 1] = jnp.ones_like(own_a[0])
    for j in range(group - 2, -1, -1):
        later[j] = own_b[j + 1] + own_a[j + 1][:, None, None] * later[j + 1]
        later_a[j] = own_a[j + 1] * later_a[j + 1]
    rtotal = own_b[0] + own_a[0][:, None, None] * later[0]
    before, after = group_scan(
        packed(total_a, total), packed(total_a, rtotal), axis, group
    )
    before = before[:, :rows]
    after = after[:, :rows]
    result = jnp.stack(
        [
            jnp.concatenate(
                [
                    excl_a[j][:, None, None] * before + excl[j],
                    later[j] + later_a[j][:, None, None] * after,
                ],
                axis=1,
            )
            for j in range(group)
        ]
    )
    full = row_exchange(result, axis, group).reshape(heads, 2 * rows, cols)
    return full[:, :rows], full[:, rows:], extra


def digit_sum(value, axis, step, radix):
    count = lax.axis_size(axis)
    digit = (lax.axis_index(axis) // step) % radix
    got = [value]
    for k in range(1, radix):
        got.append(lax.ppermute(value, axis, [(i, i ^ (k * step)) for i in range(count)]))
    total = lax.select_n(digit, *got)
    for m in range(1, radix):
        total = total + lax.select_n(digit ^ m, *got)
    return total


def all_sum(value, axes):
    for axis in axes:
        count = lax.axis_size(axis)
        step = 1
        while step < count:
            radix = 4 if count % (step * 4) == 0 else 2
            value = digit_sum(value, axis, step, radix)
            step *= radix
    return value


def block_mask_list(head_decay_rate, cutoff_list, row_position, start_list):
    is_start = jnp.any(row_position[:, None] == start_list[None, :], axis=1)
    seg_local = jnp.cumsum(is_start.astype(jnp.int32))
    begin = jnp.max(
        jnp.where(start_list[None, :] <= row_position[:, None], start_list[None, :], 0), axis=1
    )
    position = (row_position - begin).astype(jnp.float32)
    logarithm_step = (
        cutoff_list.astype(jnp.float32)[:, None] * cutoff_logarithm - head_decay_rate[None, :]
    )
    cum_log = jnp.cumsum(logarithm_step, axis=0)
    carry_in = jnp.where((seg_local == 0)[:, None], jnp.exp(cum_log), 0.0)
    carry_out = jnp.where(
        (seg_local == seg_local[-1])[:, None], jnp.exp(cum_log[-1][None, :] - cum_log), 0.0
    )
    decay_all = jnp.where(seg_local[-1] == 0, jnp.exp(cum_log[-1]), 0.0)
    return (cum_log, seg_local, position, carry_in, carry_out, decay_all)


def weights_of(cum_log, seg_local):
    count = seg_local.shape[0]
    index = jnp.arange(count, dtype=jnp.int32)
    allowed = (seg_local[:, None] == seg_local[None, :]) & (index[:, None] >= index[None, :])
    spread = cum_log.T[:, :, None] - cum_log.T[:, None, :]
    return jnp.where(allowed[None], jnp.exp(jnp.where(allowed[None], spread, 0.0)), 0.0)


def on_device(
    queries, keys, values, output_gradient, document_lengths, cutoff_rows, head_decay_rate
):
    row_count = queries.shape[1]
    query_block = queries.reshape(row_count, HEADS, HEAD_DIM)
    key_block = keys.reshape(row_count, HEADS, HEAD_DIM)
    value_block = values.reshape(row_count, HEADS, HEAD_DIM)
    gradient_block = output_gradient.reshape(row_count, HEADS, HEAD_DIM)
    block_piece = lax.axis_index("seq")
    row_position = block_piece * row_count + jnp.arange(row_count, dtype=jnp.int32)
    length_list = document_lengths[0]
    start_list = jnp.cumsum(length_list) - length_list
    cum_log, seg_local, position, carry_in, carry_out, decay_all = block_mask_list(
        head_decay_rate, cutoff_rows[0], row_position, start_list
    )
    key_f = key_block.astype(jnp.float32)
    value_f = value_block.astype(jnp.float32)
    grad_f = gradient_block.astype(jnp.float32)
    query_f = query_block.astype(jnp.float32)
    state_local = jnp.einsum(
        "the,thf->hef", carry_out[:, :, None] * key_f, value_f, precision=state_mode
    )
    back_local = jnp.einsum(
        "she,shf->hef", carry_in[:, :, None] * query_f, grad_f, precision=state_mode
    )
    state_input, backward_input, (key_scale, query_scale) = carried_both(
        decay_all,
        state_local,
        back_local,
        "seq",
        (position[:, None] * carry_out, position[:, None] * carry_in),
    )
    weight = weights_of(cum_log, seg_local)
    scores = jnp.einsum("she,the->hst", query_block, key_block, preferred_element_type=jnp.float32)
    grad_scores = jnp.einsum(
        "shf,thf->hst", gradient_block, value_block, preferred_element_type=jnp.float32
    )
    attn_prob = (weight * scores).astype(jnp.bfloat16)
    grad_prob = (weight * grad_scores).astype(jnp.bfloat16)
    value_full = jnp.einsum(
        "hst,shf->thf", attn_prob, gradient_block, preferred_element_type=jnp.float32
    )
    value_full = value_full + carry_out[:, :, None] * jnp.einsum(
        "the,hef->thf", key_f, backward_input, precision=state_mode
    )
    query_local = jnp.einsum(
        "hst,the->she", grad_prob, key_block, preferred_element_type=jnp.float32
    )
    key_local = jnp.einsum(
        "hst,she->the", grad_prob, query_block, preferred_element_type=jnp.float32
    )
    local_step = jnp.sum(key_f * key_local, axis=2) - jnp.sum(query_f * query_local, axis=2)
    rate_local = jnp.sum(position[:, None] * local_step, axis=0)
    key_moment = jnp.einsum(
        "the,thf->hef", key_scale[:, :, None] * key_f, value_f, precision=state_mode
    )
    query_moment = jnp.einsum(
        "she,shf->hef", query_scale[:, :, None] * query_f, grad_f, precision=state_mode
    )
    rate_part = (
        rate_local
        + jnp.sum(key_moment * backward_input, axis=(1, 2))
        - jnp.sum(query_moment * state_input, axis=(1, 2))
    )
    query_full = query_local + carry_in[:, :, None] * jnp.einsum(
        "shf,hef->she", grad_f, state_input, precision=state_mode
    )
    key_full = key_local + carry_out[:, :, None] * jnp.einsum(
        "thf,hef->the", value_f, backward_input, precision=state_mode
    )
    rate_total = all_sum(rate_part, ("seq", "dp"))
    token_total = row_count * lax.axis_size("seq") * lax.axis_size("dp")
    rate_grad = head_decay_rate * rate_total / math.sqrt(token_total)
    out_shape = (1, row_count, HEADS * HEAD_DIM)
    return (
        query_full.astype(jnp.bfloat16).reshape(out_shape),
        key_full.astype(jnp.bfloat16).reshape(out_shape),
        value_full.astype(jnp.bfloat16).reshape(out_shape),
        rate_grad,
    )


def solution(mesh):
    in_specs = (
        P("dp", "seq", None),
        P("dp", "seq", None),
        P("dp", "seq", None),
        P("dp", "seq", None),
        P("dp", None),
        P("dp", "seq"),
        P(),
    )
    out_specs = (P("dp", "seq", None), P("dp", "seq", None), P("dp", "seq", None), P())
    return jax.shard_map(
        on_device, mesh=mesh, in_specs=in_specs, out_specs=out_specs, check_vma=False
    )
```

```python
import math

import jax
import jax.numpy as jnp
from jax import lax
from jax.sharding import PartitionSpec as P

HEADS = 16
HEAD_DIM = 128


cutoff_logarithm = math.log(0.7)
state_mode = lax.Precision.HIGH


def packed(decay, state):
    pad = jnp.broadcast_to(decay[:, None, None], (state.shape[0], 8, state.shape[2]))
    return jnp.concatenate([state, pad], axis=1)


def combine(far, near):
    rows = far.shape[1] - 8
    state = near[:, rows : rows + 1, 0:1] * far[:, :rows] + near[:, :rows]
    return jnp.concatenate([state, far[:, rows:] * near[:, rows:]], axis=1)


def group_scan(fwd, bwd, axis, stride):
    count = lax.axis_size(axis)
    excl = jnp.concatenate([jnp.zeros_like(fwd[:, :-8]), jnp.ones_like(fwd[:, -8:])], axis=1)
    rexcl = excl
    shift = stride
    while shift < count:
        up = [(i, i + shift) for i in range(count - shift)]
        down = [(i + shift, i) for i in range(count - shift)]
        if 2 * shift >= count:
            place = lax.axis_index(axis)
            sent = jnp.where(place < count - shift, fwd, bwd)
            got = lax.ppermute(sent, axis, up + down)
            excl = jnp.where(place >= shift, combine(got, excl), excl)
            rexcl = jnp.where(place < count - shift, combine(got, rexcl), rexcl)
            break
        got = lax.ppermute(fwd, axis, up)
        rgot = lax.ppermute(bwd, axis, down)
        excl = combine(got, excl)
        rexcl = combine(rgot, rexcl)
        if 2 * shift < count:
            fwd = combine(got, fwd)
            bwd = combine(rgot, bwd)
        shift *= 2
    return excl, rexcl


def row_exchange(parts, axis, group):
    count = lax.axis_size(axis)
    place = lax.axis_index(axis) % group
    got = [lax.dynamic_index_in_dim(parts, place, 0, False)]
    for step in range(1, group):
        pairs = [
            (base + j, base + (j + step) % group)
            for base in range(0, count, group)
            for j in range(group)
        ]
        send = lax.dynamic_index_in_dim(parts, (place + step) % group, 0, False)
        got.append(lax.ppermute(send, axis, pairs))
    return jnp.stack([lax.select_n((place - j) % group, *got) for j in range(group)])


def carried_both(decay, forward_part, backward_part, axis, extra):
    count = lax.axis_size(axis)
    group = 4 if count % 4 == 0 and forward_part.shape[0] % 4 == 0 else 1
    heads, rows, cols = forward_part.shape
    share = heads // group
    pad = jnp.broadcast_to(decay[:, None, None], (heads, 8, cols))
    parts = jnp.concatenate([forward_part, backward_part, pad], axis=1)
    mine = row_exchange(parts.reshape(group, share, 2 * rows + 8, cols), axis, group)
    mine, extra = lax.optimization_barrier((mine, extra))
    own_s = mine[:, :, :rows]
    own_b = mine[:, :, rows : 2 * rows]
    own_a = mine[:, :, 2 * rows, 0]
    excl = [jnp.zeros_like(own_s[0])]
    excl_a = [jnp.ones_like(own_a[0])]
    for j in range(1, group):
        excl.append(own_a[j - 1][:, None, None] * excl[j - 1] + own_s[j - 1])
        excl_a.append(excl_a[j - 1] * own_a[j - 1])
    total = own_a[group - 1][:, None, None] * excl[group - 1] + own_s[group - 1]
    total_a = excl_a[group - 1] * own_a[group - 1]
    later = [None] * group
    later_a = [None] * group
    later[group - 1] = jnp.zeros_like(own_b[0])
    later_a[group - 1] = jnp.ones_like(own_a[0])
    for j in range(group - 2, -1, -1):
        later[j] = own_b[j + 1] + own_a[j + 1][:, None, None] * later[j + 1]
        later_a[j] = own_a[j + 1] * later_a[j + 1]
    rtotal = own_b[0] + own_a[0][:, None, None] * later[0]
    before, after = group_scan(
        packed(total_a, total), packed(total_a, rtotal), axis, group
    )
    before = before[:, :rows]
    after = after[:, :rows]
    result = jnp.stack(
        [
            jnp.concatenate(
                [
                    excl_a[j][:, None, None] * before + excl[j],
                    later[j] + later_a[j][:, None, None] * after,
                ],
                axis=1,
            )
            for j in range(group)
        ]
    )
    full = row_exchange(result, axis, group).reshape(heads, 2 * rows, cols)
    return full[:, :rows], full[:, rows:], extra


def digit_sum(value, axis, step, radix):
    count = lax.axis_size(axis)
    digit = (lax.axis_index(axis) // step) % radix
    got = [value]
    for k in range(1, radix):
        got.append(lax.ppermute(value, axis, [(i, i ^ (k * step)) for i in range(count)]))
    total = lax.select_n(digit, *got)
    for m in range(1, radix):
        total = total + lax.select_n(digit ^ m, *got)
    return total


def all_sum(value, axes):
    for axis in axes:
        count = lax.axis_size(axis)
        step = 1
        while step < count:
            radix = 4 if count % (step * 4) == 0 else 2
            value = digit_sum(value, axis, step, radix)
            step *= radix
    return value


def block_mask_list(head_decay_rate, cutoff_list, row_position, start_list):
    is_start = jnp.any(row_position[:, None] == start_list[None, :], axis=1)
    seg_local = jnp.cumsum(is_start.astype(jnp.int32))
    begin = jnp.max(
        jnp.where(start_list[None, :] <= row_position[:, None], start_list[None, :], 0), axis=1
    )
    position = (row_position - begin).astype(jnp.float32)
    logarithm_step = (
        cutoff_list.astype(jnp.float32)[:, None] * cutoff_logarithm - head_decay_rate[None, :]
    )
    cum_log = jnp.cumsum(logarithm_step, axis=0)
    carry_in = jnp.where((seg_local == 0)[:, None], jnp.exp(cum_log), 0.0)
    carry_out = jnp.where(
        (seg_local == seg_local[-1])[:, None], jnp.exp(cum_log[-1][None, :] - cum_log), 0.0
    )
    decay_all = jnp.where(seg_local[-1] == 0, jnp.exp(cum_log[-1]), 0.0)
    return (cum_log, seg_local, position, carry_in, carry_out, decay_all)


def weights_of(cum_log, seg_local):
    count = seg_local.shape[0]
    index = jnp.arange(count, dtype=jnp.int32)
    allowed = (seg_local[:, None] == seg_local[None, :]) & (index[:, None] >= index[None, :])
    spread = cum_log.T[:, :, None] - cum_log.T[:, None, :]
    return jnp.where(allowed[None], jnp.exp(jnp.where(allowed[None], spread, 0.0)), 0.0)


def on_device(
    queries, keys, values, output_gradient, document_lengths, cutoff_rows, head_decay_rate
):
    row_count = queries.shape[1]
    query_block = queries.reshape(row_count, HEADS, HEAD_DIM)
    key_block = keys.reshape(row_count, HEADS, HEAD_DIM)
    value_block = values.reshape(row_count, HEADS, HEAD_DIM)
    gradient_block = output_gradient.reshape(row_count, HEADS, HEAD_DIM)
    block_piece = lax.axis_index("seq")
    row_position = block_piece * row_count + jnp.arange(row_count, dtype=jnp.int32)
    length_list = document_lengths[0]
    start_list = jnp.cumsum(length_list) - length_list
    cum_log, seg_local, position, carry_in, carry_out, decay_all = block_mask_list(
        head_decay_rate, cutoff_rows[0], row_position, start_list
    )
    key_f = key_block.astype(jnp.float32)
    value_f = value_block.astype(jnp.float32)
    grad_f = gradient_block.astype(jnp.float32)
    query_f = query_block.astype(jnp.float32)
    state_local = jnp.einsum(
        "the,thf->hef", carry_out[:, :, None] * key_f, value_f, precision=state_mode
    )
    back_local = jnp.einsum(
        "she,shf->hef", carry_in[:, :, None] * query_f, grad_f, precision=state_mode
    )
    state_input, backward_input, tied = carried_both(
        decay_all,
        state_local,
        back_local,
        "seq",
        (
            position[:, None] * carry_out,
            position[:, None] * carry_in,
            query_block,
            key_block,
            value_block,
            gradient_block,
            cum_log,
        ),
    )
    key_scale, query_scale, query_block, key_block, value_block, gradient_block, cum_log = tied
    key_f = key_block.astype(jnp.float32)
    value_f = value_block.astype(jnp.float32)
    grad_f = gradient_block.astype(jnp.float32)
    query_f = query_block.astype(jnp.float32)
    weight = weights_of(cum_log, seg_local)
    scores = jnp.einsum("she,the->hst", query_block, key_block, preferred_element_type=jnp.float32)
    grad_scores = jnp.einsum(
        "shf,thf->hst", gradient_block, value_block, preferred_element_type=jnp.float32
    )
    attn_prob = (weight * scores).astype(jnp.bfloat16)
    grad_prob = (weight * grad_scores).astype(jnp.bfloat16)
    value_full = jnp.einsum(
        "hst,shf->thf", attn_prob, gradient_block, preferred_element_type=jnp.float32
    )
    value_full = value_full + carry_out[:, :, None] * jnp.einsum(
        "the,hef->thf", key_f, backward_input, precision=state_mode
    )
    query_local = jnp.einsum(
        "hst,the->she", grad_prob, key_block, preferred_element_type=jnp.float32
    )
    key_local = jnp.einsum(
        "hst,she->the", grad_prob, query_block, preferred_element_type=jnp.float32
    )
    local_step = jnp.sum(key_f * key_local, axis=2) - jnp.sum(query_f * query_local, axis=2)
    rate_local = jnp.sum(position[:, None] * local_step, axis=0)
    key_moment = jnp.einsum(
        "the,thf->hef", key_scale[:, :, None] * key_f, value_f, precision=state_mode
    )
    query_moment = jnp.einsum(
        "she,shf->hef", query_scale[:, :, None] * query_f, grad_f, precision=state_mode
    )
    rate_part = (
        rate_local
        + jnp.sum(key_moment * backward_input, axis=(1, 2))
        - jnp.sum(query_moment * state_input, axis=(1, 2))
    )
    query_full = query_local + carry_in[:, :, None] * jnp.einsum(
        "shf,hef->she", grad_f, state_input, precision=state_mode
    )
    key_full = key_local + carry_out[:, :, None] * jnp.einsum(
        "thf,hef->the", value_f, backward_input, precision=state_mode
    )
    rate_total = all_sum(rate_part, ("seq", "dp"))
    token_total = row_count * lax.axis_size("seq") * lax.axis_size("dp")
    rate_grad = head_decay_rate * rate_total / math.sqrt(token_total)
    out_shape = (1, row_count, HEADS * HEAD_DIM)
    return (
        query_full.astype(jnp.bfloat16).reshape(out_shape),
        key_full.astype(jnp.bfloat16).reshape(out_shape),
        value_full.astype(jnp.bfloat16).reshape(out_shape),
        rate_grad,
    )


def solution(mesh):
    in_specs = (
        P("dp", "seq", None),
        P("dp", "seq", None),
        P("dp", "seq", None),
        P("dp", "seq", None),
        P("dp", None),
        P("dp", "seq"),
        P(),
    )
    out_specs = (P("dp", "seq", None), P("dp", "seq", None), P("dp", "seq", None), P())
    return jax.shard_map(
        on_device, mesh=mesh, in_specs=in_specs, out_specs=out_specs, check_vma=False
    )
```

```python
import math

import jax
import jax.numpy as jnp
from jax import lax
from jax.sharding import PartitionSpec as P

HEADS = 16
HEAD_DIM = 128


cutoff_logarithm = math.log(0.7)
state_mode = lax.Precision.HIGH


def packed(decay, state):
    pad = jnp.broadcast_to(decay[:, None, None], (state.shape[0], 8, state.shape[2]))
    return jnp.concatenate([state, pad], axis=1)


def combine(far, near):
    rows = far.shape[1] - 8
    state = near[:, rows : rows + 1, 0:1] * far[:, :rows] + near[:, :rows]
    return jnp.concatenate([state, far[:, rows:] * near[:, rows:]], axis=1)


def group_scan(fwd, bwd, axis, stride):
    count = lax.axis_size(axis)
    excl = jnp.concatenate([jnp.zeros_like(fwd[:, :-8]), jnp.ones_like(fwd[:, -8:])], axis=1)
    rexcl = excl
    shift = stride
    while shift < count:
        up = [(i, i + shift) for i in range(count - shift)]
        down = [(i + shift, i) for i in range(count - shift)]
        if 2 * shift >= count:
            place = lax.axis_index(axis)
            sent = jnp.where(place < count - shift, fwd, bwd)
            got = lax.ppermute(sent, axis, up + down)
            excl = jnp.where(place >= shift, combine(got, excl), excl)
            rexcl = jnp.where(place < count - shift, combine(got, rexcl), rexcl)
            break
        got = lax.ppermute(fwd, axis, up)
        rgot = lax.ppermute(bwd, axis, down)
        excl = combine(got, excl)
        rexcl = combine(rgot, rexcl)
        if 2 * shift < count:
            fwd = combine(got, fwd)
            bwd = combine(rgot, bwd)
        shift *= 2
    return excl, rexcl


def row_exchange(parts, axis, group):
    count = lax.axis_size(axis)
    place = lax.axis_index(axis) % group
    got = [lax.dynamic_index_in_dim(parts, place, 0, False)]
    for step in range(1, group):
        pairs = [
            (base + j, base + (j + step) % group)
            for base in range(0, count, group)
            for j in range(group)
        ]
        send = lax.dynamic_index_in_dim(parts, (place + step) % group, 0, False)
        got.append(lax.ppermute(send, axis, pairs))
    return jnp.stack([lax.select_n((place - j) % group, *got) for j in range(group)])


def carried_both(decay, forward_part, backward_part, axis, extra):
    count = lax.axis_size(axis)
    group = 4 if count % 4 == 0 and forward_part.shape[0] % 4 == 0 else 1
    heads, rows, cols = forward_part.shape
    share = heads // group
    pad = jnp.broadcast_to(decay[:, None, None], (heads, 8, cols))
    parts = jnp.concatenate([forward_part, backward_part, pad], axis=1)
    mine = row_exchange(parts.reshape(group, share, 2 * rows + 8, cols), axis, group)
    own_s = mine[:, :, :rows]
    own_b = mine[:, :, rows : 2 * rows]
    own_a = mine[:, :, 2 * rows, 0]
    excl = [jnp.zeros_like(own_s[0])]
    excl_a = [jnp.ones_like(own_a[0])]
    for j in range(1, group):
        excl.append(own_a[j - 1][:, None, None] * excl[j - 1] + own_s[j - 1])
        excl_a.append(excl_a[j - 1] * own_a[j - 1])
    total = own_a[group - 1][:, None, None] * excl[group - 1] + own_s[group - 1]
    total_a = excl_a[group - 1] * own_a[group - 1]
    later = [None] * group
    later_a = [None] * group
    later[group - 1] = jnp.zeros_like(own_b[0])
    later_a[group - 1] = jnp.ones_like(own_a[0])
    for j in range(group - 2, -1, -1):
        later[j] = own_b[j + 1] + own_a[j + 1][:, None, None] * later[j + 1]
        later_a[j] = own_a[j + 1] * later_a[j + 1]
    rtotal = own_b[0] + own_a[0][:, None, None] * later[0]
    before, after = group_scan(
        packed(total_a, total), packed(total_a, rtotal), axis, group
    )
    before, after, extra = lax.optimization_barrier((before[:, :rows], after[:, :rows], extra))
    result = jnp.stack(
        [
            jnp.concatenate(
                [
                    excl_a[j][:, None, None] * before + excl[j],
                    later[j] + later_a[j][:, None, None] * after,
                ],
                axis=1,
            )
            for j in range(group)
        ]
    )
    full = row_exchange(result, axis, group).reshape(heads, 2 * rows, cols)
    return full[:, :rows], full[:, rows:], extra


def digit_sum(value, axis, step, radix):
    count = lax.axis_size(axis)
    digit = (lax.axis_index(axis) // step) % radix
    got = [value]
    for k in range(1, radix):
        got.append(lax.ppermute(value, axis, [(i, i ^ (k * step)) for i in range(count)]))
    total = lax.select_n(digit, *got)
    for m in range(1, radix):
        total = total + lax.select_n(digit ^ m, *got)
    return total


def all_sum(value, axes):
    for axis in axes:
        count = lax.axis_size(axis)
        step = 1
        while step < count:
            radix = 4 if count % (step * 4) == 0 else 2
            value = digit_sum(value, axis, step, radix)
            step *= radix
    return value


def block_mask_list(head_decay_rate, cutoff_list, row_position, start_list):
    is_start = jnp.any(row_position[:, None] == start_list[None, :], axis=1)
    seg_local = jnp.cumsum(is_start.astype(jnp.int32))
    begin = jnp.max(
        jnp.where(start_list[None, :] <= row_position[:, None], start_list[None, :], 0), axis=1
    )
    position = (row_position - begin).astype(jnp.float32)
    logarithm_step = (
        cutoff_list.astype(jnp.float32)[:, None] * cutoff_logarithm - head_decay_rate[None, :]
    )
    cum_log = jnp.cumsum(logarithm_step, axis=0)
    carry_in = jnp.where((seg_local == 0)[:, None], jnp.exp(cum_log), 0.0)
    carry_out = jnp.where(
        (seg_local == seg_local[-1])[:, None], jnp.exp(cum_log[-1][None, :] - cum_log), 0.0
    )
    decay_all = jnp.where(seg_local[-1] == 0, jnp.exp(cum_log[-1]), 0.0)
    return (cum_log, seg_local, position, carry_in, carry_out, decay_all)


def weights_of(cum_log, seg_local):
    count = seg_local.shape[0]
    index = jnp.arange(count, dtype=jnp.int32)
    allowed = (seg_local[:, None] == seg_local[None, :]) & (index[:, None] >= index[None, :])
    spread = cum_log.T[:, :, None] - cum_log.T[:, None, :]
    return jnp.where(allowed[None], jnp.exp(jnp.where(allowed[None], spread, 0.0)), 0.0)


def on_device(
    queries, keys, values, output_gradient, document_lengths, cutoff_rows, head_decay_rate
):
    row_count = queries.shape[1]
    query_block = queries.reshape(row_count, HEADS, HEAD_DIM)
    key_block = keys.reshape(row_count, HEADS, HEAD_DIM)
    value_block = values.reshape(row_count, HEADS, HEAD_DIM)
    gradient_block = output_gradient.reshape(row_count, HEADS, HEAD_DIM)
    block_piece = lax.axis_index("seq")
    row_position = block_piece * row_count + jnp.arange(row_count, dtype=jnp.int32)
    length_list = document_lengths[0]
    start_list = jnp.cumsum(length_list) - length_list
    cum_log, seg_local, position, carry_in, carry_out, decay_all = block_mask_list(
        head_decay_rate, cutoff_rows[0], row_position, start_list
    )
    key_f = key_block.astype(jnp.float32)
    value_f = value_block.astype(jnp.float32)
    grad_f = gradient_block.astype(jnp.float32)
    query_f = query_block.astype(jnp.float32)
    state_local = jnp.einsum(
        "the,thf->hef", carry_out[:, :, None] * key_f, value_f, precision=state_mode
    )
    back_local = jnp.einsum(
        "she,shf->hef", carry_in[:, :, None] * query_f, grad_f, precision=state_mode
    )
    state_input, backward_input, tied = carried_both(
        decay_all,
        state_local,
        back_local,
        "seq",
        (
            position[:, None] * carry_out,
            position[:, None] * carry_in,
            query_block,
            key_block,
            value_block,
            gradient_block,
            cum_log,
        ),
    )
    key_scale, query_scale, query_block, key_block, value_block, gradient_block, cum_log = tied
    key_f = key_block.astype(jnp.float32)
    value_f = value_block.astype(jnp.float32)
    grad_f = gradient_block.astype(jnp.float32)
    query_f = query_block.astype(jnp.float32)
    weight = weights_of(cum_log, seg_local)
    scores = jnp.einsum("she,the->hst", query_block, key_block, preferred_element_type=jnp.float32)
    grad_scores = jnp.einsum(
        "shf,thf->hst", gradient_block, value_block, preferred_element_type=jnp.float32
    )
    attn_prob = (weight * scores).astype(jnp.bfloat16)
    grad_prob = (weight * grad_scores).astype(jnp.bfloat16)
    value_full = jnp.einsum(
        "hst,shf->thf", attn_prob, gradient_block, preferred_element_type=jnp.float32
    )
    value_full = value_full + carry_out[:, :, None] * jnp.einsum(
        "the,hef->thf", key_f, backward_input, precision=state_mode
    )
    query_local = jnp.einsum(
        "hst,the->she", grad_prob, key_block, preferred_element_type=jnp.float32
    )
    key_local = jnp.einsum(
        "hst,she->the", grad_prob, query_block, preferred_element_type=jnp.float32
    )
    local_step = jnp.sum(key_f * key_local, axis=2) - jnp.sum(query_f * query_local, axis=2)
    rate_local = jnp.sum(position[:, None] * local_step, axis=0)
    key_moment = jnp.einsum(
        "the,thf->hef", key_scale[:, :, None] * key_f, value_f, precision=state_mode
    )
    query_moment = jnp.einsum(
        "she,shf->hef", query_scale[:, :, None] * query_f, grad_f, precision=state_mode
    )
    rate_part = (
        rate_local
        + jnp.sum(key_moment * backward_input, axis=(1, 2))
        - jnp.sum(query_moment * state_input, axis=(1, 2))
    )
    query_full = query_local + carry_in[:, :, None] * jnp.einsum(
        "shf,hef->she", grad_f, state_input, precision=state_mode
    )
    key_full = key_local + carry_out[:, :, None] * jnp.einsum(
        "thf,hef->the", value_f, backward_input, precision=state_mode
    )
    rate_total = all_sum(rate_part, ("seq", "dp"))
    token_total = row_count * lax.axis_size("seq") * lax.axis_size("dp")
    rate_grad = head_decay_rate * rate_total / math.sqrt(token_total)
    out_shape = (1, row_count, HEADS * HEAD_DIM)
    return (
        query_full.astype(jnp.bfloat16).reshape(out_shape),
        key_full.astype(jnp.bfloat16).reshape(out_shape),
        value_full.astype(jnp.bfloat16).reshape(out_shape),
        rate_grad,
    )


def solution(mesh):
    in_specs = (
        P("dp", "seq", None),
        P("dp", "seq", None),
        P("dp", "seq", None),
        P("dp", "seq", None),
        P("dp", None),
        P("dp", "seq"),
        P(),
    )
    out_specs = (P("dp", "seq", None), P("dp", "seq", None), P("dp", "seq", None), P())
    return jax.shard_map(
        on_device, mesh=mesh, in_specs=in_specs, out_specs=out_specs, check_vma=False
    )
```

```python
import math

import jax
import jax.numpy as jnp
from jax import lax
from jax.sharding import PartitionSpec as P

HEADS = 16
HEAD_DIM = 128


cutoff_logarithm = math.log(0.7)
state_mode = lax.Precision.HIGH


def packed(decay, state):
    pad = jnp.broadcast_to(decay[:, None, None], (state.shape[0], 8, state.shape[2]))
    return jnp.concatenate([state, pad], axis=1)


def combine(far, near):
    rows = far.shape[1] - 8
    state = near[:, rows : rows + 1, 0:1] * far[:, :rows] + near[:, :rows]
    return jnp.concatenate([state, far[:, rows:] * near[:, rows:]], axis=1)


def group_scan(fwd, bwd, axis, stride):
    count = lax.axis_size(axis)
    excl = jnp.concatenate([jnp.zeros_like(fwd[:, :-8]), jnp.ones_like(fwd[:, -8:])], axis=1)
    rexcl = excl
    shift = stride
    while shift < count:
        up = [(i, i + shift) for i in range(count - shift)]
        down = [(i + shift, i) for i in range(count - shift)]
        if 2 * shift >= count:
            place = lax.axis_index(axis)
            sent = jnp.where(place < count - shift, fwd, bwd)
            got = lax.ppermute(sent, axis, up + down)
            excl = jnp.where(place >= shift, combine(got, excl), excl)
            rexcl = jnp.where(place < count - shift, combine(got, rexcl), rexcl)
            break
        got = lax.ppermute(fwd, axis, up)
        rgot = lax.ppermute(bwd, axis, down)
        excl = combine(got, excl)
        rexcl = combine(rgot, rexcl)
        if 2 * shift < count:
            fwd = combine(got, fwd)
            bwd = combine(rgot, bwd)
        shift *= 2
    return excl, rexcl


def row_exchange(parts, axis, group):
    count = lax.axis_size(axis)
    place = lax.axis_index(axis) % group
    got = [lax.dynamic_index_in_dim(parts, place, 0, False)]
    for step in range(1, group):
        pairs = [
            (base + j, base + (j + step) % group)
            for base in range(0, count, group)
            for j in range(group)
        ]
        send = lax.dynamic_index_in_dim(parts, (place + step) % group, 0, False)
        got.append(lax.ppermute(send, axis, pairs))
    return jnp.stack([lax.select_n((place - j) % group, *got) for j in range(group)])


def carried_both(decay, forward_part, backward_part, axis, extra):
    count = lax.axis_size(axis)
    group = 4 if count % 4 == 0 and forward_part.shape[0] % 4 == 0 else 1
    heads, rows, cols = forward_part.shape
    share = heads // group
    pad = jnp.broadcast_to(decay[:, None, None], (heads, 8, cols))
    parts = jnp.concatenate([forward_part, backward_part, pad], axis=1)
    mine = row_exchange(parts.reshape(group, share, 2 * rows + 8, cols), axis, group)
    own_s = mine[:, :, :rows]
    own_b = mine[:, :, rows : 2 * rows]
    own_a = mine[:, :, 2 * rows, 0]
    excl = [jnp.zeros_like(own_s[0])]
    excl_a = [jnp.ones_like(own_a[0])]
    for j in range(1, group):
        excl.append(own_a[j - 1][:, None, None] * excl[j - 1] + own_s[j - 1])
        excl_a.append(excl_a[j - 1] * own_a[j - 1])
    total = own_a[group - 1][:, None, None] * excl[group - 1] + own_s[group - 1]
    total_a = excl_a[group - 1] * own_a[group - 1]
    later = [None] * group
    later_a = [None] * group
    later[group - 1] = jnp.zeros_like(own_b[0])
    later_a[group - 1] = jnp.ones_like(own_a[0])
    for j in range(group - 2, -1, -1):
        later[j] = own_b[j + 1] + own_a[j + 1][:, None, None] * later[j + 1]
        later_a[j] = own_a[j + 1] * later_a[j + 1]
    rtotal = own_b[0] + own_a[0][:, None, None] * later[0]
    before, after = group_scan(
        packed(total_a, total), packed(total_a, rtotal), axis, group
    )
    before, after, extra = lax.optimization_barrier((before[:, :rows], after[:, :rows], extra))
    result = jnp.stack(
        [
            jnp.concatenate(
                [
                    excl_a[j][:, None, None] * before + excl[j],
                    later[j] + later_a[j][:, None, None] * after,
                ],
                axis=1,
            )
            for j in range(group)
        ]
    )
    full = row_exchange(result, axis, group).reshape(heads, 2 * rows, cols)
    return full[:, :rows], full[:, rows:], extra


def digit_sum(value, axis, step, radix):
    count = lax.axis_size(axis)
    digit = (lax.axis_index(axis) // step) % radix
    got = [value]
    for k in range(1, radix):
        got.append(lax.ppermute(value, axis, [(i, i ^ (k * step)) for i in range(count)]))
    total = lax.select_n(digit, *got)
    for m in range(1, radix):
        total = total + lax.select_n(digit ^ m, *got)
    return total


def all_sum(value, axes):
    for axis in axes:
        count = lax.axis_size(axis)
        step = 1
        while step < count:
            radix = 4 if count % (step * 4) == 0 else 2
            value = digit_sum(value, axis, step, radix)
            step *= radix
    return value


def block_mask_list(head_decay_rate, cutoff_list, row_position, start_list):
    is_start = jnp.any(row_position[:, None] == start_list[None, :], axis=1)
    seg_local = jnp.cumsum(is_start.astype(jnp.int32))
    begin = jnp.max(
        jnp.where(start_list[None, :] <= row_position[:, None], start_list[None, :], 0), axis=1
    )
    position = (row_position - begin).astype(jnp.float32)
    logarithm_step = (
        cutoff_list.astype(jnp.float32)[:, None] * cutoff_logarithm - head_decay_rate[None, :]
    )
    cum_log = jnp.cumsum(logarithm_step, axis=0)
    carry_in = jnp.where((seg_local == 0)[:, None], jnp.exp(cum_log), 0.0)
    carry_out = jnp.where(
        (seg_local == seg_local[-1])[:, None], jnp.exp(cum_log[-1][None, :] - cum_log), 0.0
    )
    decay_all = jnp.where(seg_local[-1] == 0, jnp.exp(cum_log[-1]), 0.0)
    return (cum_log, seg_local, position, carry_in, carry_out, decay_all)


def weights_of(cum_log, seg_local):
    count = seg_local.shape[0]
    index = jnp.arange(count, dtype=jnp.int32)
    allowed = (seg_local[:, None] == seg_local[None, :]) & (index[:, None] >= index[None, :])
    spread = cum_log.T[:, :, None] - cum_log.T[:, None, :]
    return jnp.where(allowed[None], jnp.exp(jnp.where(allowed[None], spread, 0.0)), 0.0)


def on_device(
    queries, keys, values, output_gradient, document_lengths, cutoff_rows, head_decay_rate
):
    row_count = queries.shape[1]
    query_block = queries.reshape(row_count, HEADS, HEAD_DIM)
    key_block = keys.reshape(row_count, HEADS, HEAD_DIM)
    value_block = values.reshape(row_count, HEADS, HEAD_DIM)
    gradient_block = output_gradient.reshape(row_count, HEADS, HEAD_DIM)
    block_piece = lax.axis_index("seq")
    row_position = block_piece * row_count + jnp.arange(row_count, dtype=jnp.int32)
    length_list = document_lengths[0]
    start_list = jnp.cumsum(length_list) - length_list
    cum_log, seg_local, position, carry_in, carry_out, decay_all = block_mask_list(
        head_decay_rate, cutoff_rows[0], row_position, start_list
    )
    key_f = key_block.astype(jnp.float32)
    value_f = value_block.astype(jnp.float32)
    grad_f = gradient_block.astype(jnp.float32)
    query_f = query_block.astype(jnp.float32)
    state_local = jnp.einsum(
        "the,thf->hef", carry_out[:, :, None] * key_f, value_f, precision=state_mode
    )
    back_local = jnp.einsum(
        "she,shf->hef", carry_in[:, :, None] * query_f, grad_f, precision=state_mode
    )
    state_input, backward_input, tied = carried_both(
        decay_all,
        state_local,
        back_local,
        "seq",
        (
            position[:, None] * carry_out,
            position[:, None] * carry_in,
            query_block,
            key_block,
            value_block,
            gradient_block,
            cum_log,
        ),
    )
    key_scale, query_scale, query_block, key_block, value_block, gradient_block, cum_log = tied
    key_f = key_block.astype(jnp.float32)
    value_f = value_block.astype(jnp.float32)
    grad_f = gradient_block.astype(jnp.float32)
    query_f = query_block.astype(jnp.float32)
    weight = weights_of(cum_log, seg_local)
    scores = jnp.einsum("she,the->hst", query_block, key_block, preferred_element_type=jnp.float32)
    grad_scores = jnp.einsum(
        "shf,thf->hst", gradient_block, value_block, preferred_element_type=jnp.float32
    )
    attn_prob = (weight * scores).astype(jnp.bfloat16)
    grad_prob = (weight * grad_scores).astype(jnp.bfloat16)
    query_local = jnp.einsum(
        "hst,the->she", grad_prob, key_block, preferred_element_type=jnp.float32
    )
    key_local = jnp.einsum(
        "hst,she->the", grad_prob, query_block, preferred_element_type=jnp.float32
    )
    value_local = jnp.einsum(
        "hst,shf->thf", attn_prob, gradient_block, preferred_element_type=jnp.float32
    )
    query_local, key_local, value_local = lax.optimization_barrier(
        (query_local, key_local, value_local)
    )
    local_step = jnp.sum(key_f * key_local, axis=2) - jnp.sum(query_f * query_local, axis=2)
    rate_local = jnp.sum(position[:, None] * local_step, axis=0)
    key_moment = jnp.einsum(
        "the,thf->hef", key_scale[:, :, None] * key_f, value_f, precision=state_mode
    )
    query_moment = jnp.einsum(
        "she,shf->hef", query_scale[:, :, None] * query_f, grad_f, precision=state_mode
    )
    rate_part = (
        rate_local
        + jnp.sum(key_moment * backward_input, axis=(1, 2))
        - jnp.sum(query_moment * state_input, axis=(1, 2))
    )
    query_full = query_local + carry_in[:, :, None] * jnp.einsum(
        "shf,hef->she", grad_f, state_input, precision=state_mode
    )
    key_full = key_local + carry_out[:, :, None] * jnp.einsum(
        "thf,hef->the", value_f, backward_input, precision=state_mode
    )
    value_full = value_local + carry_out[:, :, None] * jnp.einsum(
        "the,hef->thf", key_f, backward_input, precision=state_mode
    )
    rate_total = all_sum(rate_part, ("seq", "dp"))
    token_total = row_count * lax.axis_size("seq") * lax.axis_size("dp")
    rate_grad = head_decay_rate * rate_total / math.sqrt(token_total)
    out_shape = (1, row_count, HEADS * HEAD_DIM)
    return (
        query_full.astype(jnp.bfloat16).reshape(out_shape),
        key_full.astype(jnp.bfloat16).reshape(out_shape),
        value_full.astype(jnp.bfloat16).reshape(out_shape),
        rate_grad,
    )


def solution(mesh):
    in_specs = (
        P("dp", "seq", None),
        P("dp", "seq", None),
        P("dp", "seq", None),
        P("dp", "seq", None),
        P("dp", None),
        P("dp", "seq"),
        P(),
    )
    out_specs = (P("dp", "seq", None), P("dp", "seq", None), P("dp", "seq", None), P())
    return jax.shard_map(
        on_device, mesh=mesh, in_specs=in_specs, out_specs=out_specs, check_vma=False
    )
```

```python
import math

import jax
import jax.numpy as jnp
from jax import lax
from jax.sharding import PartitionSpec as P

HEADS = 16
HEAD_DIM = 128


cutoff_logarithm = math.log(0.7)
state_mode = lax.Precision.HIGH


def packed(decay, state):
    pad = jnp.broadcast_to(decay[:, None, None], (state.shape[0], 8, state.shape[2]))
    return jnp.concatenate([state, pad], axis=1)


def combine(far, near):
    rows = far.shape[1] - 8
    state = near[:, rows : rows + 1, 0:1] * far[:, :rows] + near[:, :rows]
    return jnp.concatenate([state, far[:, rows:] * near[:, rows:]], axis=1)


def group_scan(fwd, bwd, axis, stride):
    count = lax.axis_size(axis)
    excl = jnp.concatenate([jnp.zeros_like(fwd[:, :-8]), jnp.ones_like(fwd[:, -8:])], axis=1)
    rexcl = excl
    shift = stride
    while shift < count:
        up = [(i, i + shift) for i in range(count - shift)]
        down = [(i + shift, i) for i in range(count - shift)]
        if 2 * shift >= count:
            place = lax.axis_index(axis)
            sent = jnp.where(place < count - shift, fwd, bwd)
            got = lax.ppermute(sent, axis, up + down)
            excl = jnp.where(place >= shift, combine(got, excl), excl)
            rexcl = jnp.where(place < count - shift, combine(got, rexcl), rexcl)
            break
        got = lax.ppermute(fwd, axis, up)
        rgot = lax.ppermute(bwd, axis, down)
        excl = combine(got, excl)
        rexcl = combine(rgot, rexcl)
        if 2 * shift < count:
            fwd = combine(got, fwd)
            bwd = combine(rgot, bwd)
        shift *= 2
    return excl, rexcl


def row_exchange(parts, axis, group):
    count = lax.axis_size(axis)
    place = lax.axis_index(axis) % group
    got = [lax.dynamic_index_in_dim(parts, place, 0, False)]
    for step in range(1, group):
        pairs = [
            (base + j, base + (j + step) % group)
            for base in range(0, count, group)
            for j in range(group)
        ]
        send = lax.dynamic_index_in_dim(parts, (place + step) % group, 0, False)
        got.append(lax.ppermute(send, axis, pairs))
    return jnp.stack([lax.select_n((place - j) % group, *got) for j in range(group)])


def carried_both(decay, forward_part, backward_part, axis):
    count = lax.axis_size(axis)
    group = 4 if count % 4 == 0 and forward_part.shape[0] % 4 == 0 else 1
    heads, rows, cols = forward_part.shape
    share = heads // group
    pad = jnp.broadcast_to(decay[:, None, None], (heads, 8, cols))
    parts = jnp.concatenate([forward_part, backward_part, pad], axis=1)
    mine = row_exchange(parts.reshape(group, share, 2 * rows + 8, cols), axis, group)
    own_s = mine[:, :, :rows]
    own_b = mine[:, :, rows : 2 * rows]
    own_a = mine[:, :, 2 * rows, 0]
    excl = [jnp.zeros_like(own_s[0])]
    excl_a = [jnp.ones_like(own_a[0])]
    for j in range(1, group):
        excl.append(own_a[j - 1][:, None, None] * excl[j - 1] + own_s[j - 1])
        excl_a.append(excl_a[j - 1] * own_a[j - 1])
    total = own_a[group - 1][:, None, None] * excl[group - 1] + own_s[group - 1]
    total_a = excl_a[group - 1] * own_a[group - 1]
    later = [None] * group
    later_a = [None] * group
    later[group - 1] = jnp.zeros_like(own_b[0])
    later_a[group - 1] = jnp.ones_like(own_a[0])
    for j in range(group - 2, -1, -1):
        later[j] = own_b[j + 1] + own_a[j + 1][:, None, None] * later[j + 1]
        later_a[j] = own_a[j + 1] * later_a[j + 1]
    rtotal = own_b[0] + own_a[0][:, None, None] * later[0]
    before, after = group_scan(
        packed(total_a, total), packed(total_a, rtotal), axis, group
    )
    before = before[:, :rows]
    after = after[:, :rows]
    result = jnp.stack(
        [
            jnp.concatenate(
                [
                    excl_a[j][:, None, None] * before + excl[j],
                    later[j] + later_a[j][:, None, None] * after,
                ],
                axis=1,
            )
            for j in range(group)
        ]
    )
    full = row_exchange(result, axis, group).reshape(heads, 2 * rows, cols)
    return full[:, :rows], full[:, rows:]


def digit_sum(value, axis, step, radix):
    count = lax.axis_size(axis)
    digit = (lax.axis_index(axis) // step) % radix
    got = [value]
    for k in range(1, radix):
        got.append(lax.ppermute(value, axis, [(i, i ^ (k * step)) for i in range(count)]))
    total = lax.select_n(digit, *got)
    for m in range(1, radix):
        total = total + lax.select_n(digit ^ m, *got)
    return total


def all_sum(value, axes):
    for axis in axes:
        count = lax.axis_size(axis)
        step = 1
        while step < count:
            radix = 4 if count % (step * 4) == 0 else 2
            value = digit_sum(value, axis, step, radix)
            step *= radix
    return value


def block_mask_list(head_decay_rate, cutoff_list, row_position, start_list):
    is_start = jnp.any(row_position[:, None] == start_list[None, :], axis=1)
    seg_local = jnp.cumsum(is_start.astype(jnp.int32))
    begin = jnp.max(
        jnp.where(start_list[None, :] <= row_position[:, None], start_list[None, :], 0), axis=1
    )
    position = (row_position - begin).astype(jnp.float32)
    logarithm_step = (
        cutoff_list.astype(jnp.float32)[:, None] * cutoff_logarithm - head_decay_rate[None, :]
    )
    cum_log = jnp.cumsum(logarithm_step, axis=0)
    carry_in = jnp.where((seg_local == 0)[:, None], jnp.exp(cum_log), 0.0)
    carry_out = jnp.where(
        (seg_local == seg_local[-1])[:, None], jnp.exp(cum_log[-1][None, :] - cum_log), 0.0
    )
    decay_all = jnp.where(seg_local[-1] == 0, jnp.exp(cum_log[-1]), 0.0)
    return (cum_log, seg_local, position, carry_in, carry_out, decay_all)


def weights_of(cum_log, seg_local):
    count = seg_local.shape[0]
    index = jnp.arange(count, dtype=jnp.int32)
    allowed = (seg_local[:, None] == seg_local[None, :]) & (index[:, None] >= index[None, :])
    spread = cum_log.T[:, :, None] - cum_log.T[:, None, :]
    return jnp.where(allowed[None], jnp.exp(jnp.where(allowed[None], spread, 0.0)), 0.0)


def on_device(
    queries, keys, values, output_gradient, document_lengths, cutoff_rows, head_decay_rate
):
    row_count = queries.shape[1]
    query_block = queries.reshape(row_count, HEADS, HEAD_DIM)
    key_block = keys.reshape(row_count, HEADS, HEAD_DIM)
    value_block = values.reshape(row_count, HEADS, HEAD_DIM)
    gradient_block = output_gradient.reshape(row_count, HEADS, HEAD_DIM)
    block_piece = lax.axis_index("seq")
    row_position = block_piece * row_count + jnp.arange(row_count, dtype=jnp.int32)
    length_list = document_lengths[0]
    start_list = jnp.cumsum(length_list) - length_list
    cum_log, seg_local, position, carry_in, carry_out, decay_all = block_mask_list(
        head_decay_rate, cutoff_rows[0], row_position, start_list
    )
    key_f = key_block.astype(jnp.float32)
    value_f = value_block.astype(jnp.float32)
    grad_f = gradient_block.astype(jnp.float32)
    query_f = query_block.astype(jnp.float32)
    state_local = jnp.einsum(
        "the,thf->hef", carry_out[:, :, None] * key_f, value_f, precision=state_mode
    )
    back_local = jnp.einsum(
        "she,shf->hef", carry_in[:, :, None] * query_f, grad_f, precision=state_mode
    )
    state_input, backward_input = carried_both(decay_all, state_local, back_local, "seq")
    weight = weights_of(cum_log, seg_local)
    scores = jnp.einsum("she,the->hst", query_block, key_block, preferred_element_type=jnp.float32)
    grad_scores = jnp.einsum(
        "shf,thf->hst", gradient_block, value_block, preferred_element_type=jnp.float32
    )
    attn_prob = (weight * scores).astype(jnp.bfloat16)
    grad_prob = (weight * grad_scores).astype(jnp.bfloat16)
    value_full = jnp.einsum(
        "hst,shf->thf", attn_prob, gradient_block, preferred_element_type=jnp.float32
    )
    value_full = value_full + carry_out[:, :, None] * jnp.einsum(
        "the,hef->thf", key_f, backward_input, precision=state_mode
    )
    query_full = jnp.einsum(
        "hst,the->she", grad_prob, key_block, preferred_element_type=jnp.float32
    )
    query_full = query_full + carry_in[:, :, None] * jnp.einsum(
        "shf,hef->she", grad_f, state_input, precision=state_mode
    )
    key_full = jnp.einsum(
        "hst,she->the", grad_prob, query_block, preferred_element_type=jnp.float32
    )
    key_full = key_full + carry_out[:, :, None] * jnp.einsum(
        "thf,hef->the", value_f, backward_input, precision=state_mode
    )
    inner_step = jnp.sum(key_f * key_full, axis=2) - jnp.sum(query_f * query_full, axis=2)
    rate_part = jnp.sum(position[:, None] * inner_step, axis=0)
    rate_total = all_sum(rate_part, ("seq", "dp"))
    token_total = row_count * lax.axis_size("seq") * lax.axis_size("dp")
    rate_grad = head_decay_rate * rate_total / math.sqrt(token_total)
    out_shape = (1, row_count, HEADS * HEAD_DIM)
    return (
        query_full.astype(jnp.bfloat16).reshape(out_shape),
        key_full.astype(jnp.bfloat16).reshape(out_shape),
        value_full.astype(jnp.bfloat16).reshape(out_shape),
        rate_grad,
    )


def solution(mesh):
    in_specs = (
        P("dp", "seq", None),
        P("dp", "seq", None),
        P("dp", "seq", None),
        P("dp", "seq", None),
        P("dp", None),
        P("dp", "seq"),
        P(),
    )
    out_specs = (P("dp", "seq", None), P("dp", "seq", None), P("dp", "seq", None), P())
    return jax.shard_map(
        on_device, mesh=mesh, in_specs=in_specs, out_specs=out_specs, check_vma=False
    )
```

```python
import math

import jax
import jax.numpy as jnp
from jax import lax
from jax.sharding import PartitionSpec as P

HEADS = 16
HEAD_DIM = 128


cutoff_logarithm = math.log(0.7)
state_mode = lax.Precision.HIGH


def packed(decay, state):
    pad = jnp.broadcast_to(decay[:, None, None], (state.shape[0], 8, state.shape[2]))
    return jnp.concatenate([state, pad], axis=1)


def combine(far, near):
    rows = far.shape[1] - 8
    state = near[:, rows : rows + 1, 0:1] * far[:, :rows] + near[:, :rows]
    return jnp.concatenate([state, far[:, rows:] * near[:, rows:]], axis=1)


def group_scan(fwd, bwd, axis, stride):
    count = lax.axis_size(axis)
    excl = jnp.concatenate([jnp.zeros_like(fwd[:, :-8]), jnp.ones_like(fwd[:, -8:])], axis=1)
    rexcl = excl
    shift = stride
    while shift < count:
        up = [(i, i + shift) for i in range(count - shift)]
        down = [(i + shift, i) for i in range(count - shift)]
        got = lax.ppermute(fwd, axis, up)
        rgot = lax.ppermute(bwd, axis, down)
        excl = combine(got, excl)
        rexcl = combine(rgot, rexcl)
        if 2 * shift < count:
            fwd = combine(got, fwd)
            bwd = combine(rgot, bwd)
        shift *= 2
    return excl, rexcl


def row_exchange(parts, axis, group):
    count = lax.axis_size(axis)
    place = lax.axis_index(axis) % group
    got = [lax.dynamic_index_in_dim(parts, place, 0, False)]
    for step in range(1, group):
        pairs = [
            (base + j, base + (j + step) % group)
            for base in range(0, count, group)
            for j in range(group)
        ]
        send = lax.dynamic_index_in_dim(parts, (place + step) % group, 0, False)
        got.append(lax.ppermute(send, axis, pairs))
    return jnp.stack([lax.select_n((place - j) % group, *got) for j in range(group)])


def carried_both(decay, forward_part, backward_part, axis):
    count = lax.axis_size(axis)
    group = 4 if count % 4 == 0 and forward_part.shape[0] % 4 == 0 else 1
    heads, rows, cols = forward_part.shape
    share = heads // group
    pad = jnp.broadcast_to(decay[:, None, None], (heads, 8, cols))
    parts = jnp.concatenate([forward_part, backward_part, pad], axis=1)
    mine = row_exchange(parts.reshape(group, share, 2 * rows + 8, cols), axis, group)
    own_s = mine[:, :, :rows]
    own_b = mine[:, :, rows : 2 * rows]
    own_a = mine[:, :, 2 * rows, 0]
    excl = [jnp.zeros_like(own_s[0])]
    excl_a = [jnp.ones_like(own_a[0])]
    for j in range(1, group):
        excl.append(own_a[j - 1][:, None, None] * excl[j - 1] + own_s[j - 1])
        excl_a.append(excl_a[j - 1] * own_a[j - 1])
    total = own_a[group - 1][:, None, None] * excl[group - 1] + own_s[group - 1]
    total_a = excl_a[group - 1] * own_a[group - 1]
    later = [None] * group
    later_a = [None] * group
    later[group - 1] = jnp.zeros_like(own_b[0])
    later_a[group - 1] = jnp.ones_like(own_a[0])
    for j in range(group - 2, -1, -1):
        later[j] = own_b[j + 1] + own_a[j + 1][:, None, None] * later[j + 1]
        later_a[j] = own_a[j + 1] * later_a[j + 1]
    rtotal = own_b[0] + own_a[0][:, None, None] * later[0]
    before, after = group_scan(
        packed(total_a, total), packed(total_a, rtotal), axis, group
    )
    before = before[:, :rows]
    after = after[:, :rows]
    result = jnp.stack(
        [
            jnp.concatenate(
                [
                    excl_a[j][:, None, None] * before + excl[j],
                    later[j] + later_a[j][:, None, None] * after,
                ],
                axis=1,
            )
            for j in range(group)
        ]
    )
    full = row_exchange(result, axis, group).reshape(heads, 2 * rows, cols)
    return full[:, :rows], full[:, rows:]


def digit_sum(value, axes, count, step, radix):
    digit = (lax.axis_index(axes) // step) % radix
    got = [value]
    for k in range(1, radix):
        got.append(lax.ppermute(value, axes, [(i, i ^ (k * step)) for i in range(count)]))
    total = lax.select_n(digit, *got)
    for m in range(1, radix):
        total = total + lax.select_n(digit ^ m, *got)
    return total


def all_sum(value, axes):
    count = math.prod(lax.axis_size(axis) for axis in axes)
    step = 1
    while step < count:
        radix = 4 if count % (step * 4) == 0 else 2
        value = digit_sum(value, axes, count, step, radix)
        step *= radix
    return value


def block_mask_list(head_decay_rate, cutoff_list, row_position, start_list):
    is_start = jnp.any(row_position[:, None] == start_list[None, :], axis=1)
    seg_local = jnp.cumsum(is_start.astype(jnp.int32))
    begin = jnp.max(
        jnp.where(start_list[None, :] <= row_position[:, None], start_list[None, :], 0), axis=1
    )
    position = (row_position - begin).astype(jnp.float32)
    logarithm_step = (
        cutoff_list.astype(jnp.float32)[:, None] * cutoff_logarithm - head_decay_rate[None, :]
    )
    cum_log = jnp.cumsum(logarithm_step, axis=0)
    carry_in = jnp.where((seg_local == 0)[:, None], jnp.exp(cum_log), 0.0)
    carry_out = jnp.where(
        (seg_local == seg_local[-1])[:, None], jnp.exp(cum_log[-1][None, :] - cum_log), 0.0
    )
    decay_all = jnp.where(seg_local[-1] == 0, jnp.exp(cum_log[-1]), 0.0)
    return (cum_log, seg_local, position, carry_in, carry_out, decay_all)


def weights_of(cum_log, seg_local):
    count = seg_local.shape[0]
    index = jnp.arange(count, dtype=jnp.int32)
    allowed = (seg_local[:, None] == seg_local[None, :]) & (index[:, None] >= index[None, :])
    spread = cum_log.T[:, :, None] - cum_log.T[:, None, :]
    return jnp.where(allowed[None], jnp.exp(jnp.where(allowed[None], spread, 0.0)), 0.0)


def on_device(
    queries, keys, values, output_gradient, document_lengths, cutoff_rows, head_decay_rate
):
    row_count = queries.shape[1]
    query_block = queries.reshape(row_count, HEADS, HEAD_DIM)
    key_block = keys.reshape(row_count, HEADS, HEAD_DIM)
    value_block = values.reshape(row_count, HEADS, HEAD_DIM)
    gradient_block = output_gradient.reshape(row_count, HEADS, HEAD_DIM)
    block_piece = lax.axis_index("seq")
    row_position = block_piece * row_count + jnp.arange(row_count, dtype=jnp.int32)
    length_list = document_lengths[0]
    start_list = jnp.cumsum(length_list) - length_list
    cum_log, seg_local, position, carry_in, carry_out, decay_all = block_mask_list(
        head_decay_rate, cutoff_rows[0], row_position, start_list
    )
    key_f = key_block.astype(jnp.float32)
    value_f = value_block.astype(jnp.float32)
    grad_f = gradient_block.astype(jnp.float32)
    query_f = query_block.astype(jnp.float32)
    state_local = jnp.einsum(
        "the,thf->hef", carry_out[:, :, None] * key_f, value_f, precision=state_mode
    )
    back_local = jnp.einsum(
        "she,shf->hef", carry_in[:, :, None] * query_f, grad_f, precision=state_mode
    )
    state_input, backward_input = carried_both(decay_all, state_local, back_local, "seq")
    weight = weights_of(cum_log, seg_local)
    scores = jnp.einsum("she,the->hst", query_block, key_block, preferred_element_type=jnp.float32)
    grad_scores = jnp.einsum(
        "shf,thf->hst", gradient_block, value_block, preferred_element_type=jnp.float32
    )
    attn_prob = (weight * scores).astype(jnp.bfloat16)
    grad_prob = (weight * grad_scores).astype(jnp.bfloat16)
    value_full = jnp.einsum(
        "hst,shf->thf", attn_prob, gradient_block, preferred_element_type=jnp.float32
    )
    value_full = value_full + carry_out[:, :, None] * jnp.einsum(
        "the,hef->thf", key_f, backward_input, precision=state_mode
    )
    query_full = jnp.einsum(
        "hst,the->she", grad_prob, key_block, preferred_element_type=jnp.float32
    )
    query_full = query_full + carry_in[:, :, None] * jnp.einsum(
        "shf,hef->she", grad_f, state_input, precision=state_mode
    )
    key_full = jnp.einsum(
        "hst,she->the", grad_prob, query_block, preferred_element_type=jnp.float32
    )
    key_full = key_full + carry_out[:, :, None] * jnp.einsum(
        "thf,hef->the", value_f, backward_input, precision=state_mode
    )
    inner_step = jnp.sum(key_f * key_full, axis=2) - jnp.sum(query_f * query_full, axis=2)
    rate_part = jnp.sum(position[:, None] * inner_step, axis=0)
    rate_total = all_sum(rate_part, ("seq", "dp"))
    token_total = row_count * lax.axis_size("seq") * lax.axis_size("dp")
    rate_grad = head_decay_rate * rate_total / math.sqrt(token_total)
    out_shape = (1, row_count, HEADS * HEAD_DIM)
    return (
        query_full.astype(jnp.bfloat16).reshape(out_shape),
        key_full.astype(jnp.bfloat16).reshape(out_shape),
        value_full.astype(jnp.bfloat16).reshape(out_shape),
        rate_grad,
    )


def solution(mesh):
    in_specs = (
        P("dp", "seq", None),
        P("dp", "seq", None),
        P("dp", "seq", None),
        P("dp", "seq", None),
        P("dp", None),
        P("dp", "seq"),
        P(),
    )
    out_specs = (P("dp", "seq", None), P("dp", "seq", None), P("dp", "seq", None), P())
    return jax.shard_map(
        on_device, mesh=mesh, in_specs=in_specs, out_specs=out_specs, check_vma=False
    )
```

```python
import math

import jax
import jax.numpy as jnp
from jax import lax
from jax.sharding import PartitionSpec as P

HEADS = 16
HEAD_DIM = 128


cutoff_logarithm = math.log(0.7)
state_mode = lax.Precision.HIGH


def packed(decay, state):
    pad = jnp.broadcast_to(decay[:, None, None], (state.shape[0], 8, state.shape[2]))
    return jnp.concatenate([state, pad], axis=1)


def combine(far, near):
    rows = far.shape[1] - 8
    state = near[:, rows : rows + 1, 0:1] * far[:, :rows] + near[:, :rows]
    return jnp.concatenate([state, far[:, rows:] * near[:, rows:]], axis=1)


def group_scan(fwd, bwd, axis, stride):
    count = lax.axis_size(axis)
    excl = jnp.concatenate([jnp.zeros_like(fwd[:, :-8]), jnp.ones_like(fwd[:, -8:])], axis=1)
    rexcl = excl
    shift = stride
    while shift < count:
        up = [(i, i + shift) for i in range(count - shift)]
        down = [(i + shift, i) for i in range(count - shift)]
        got = lax.ppermute(fwd, axis, up)
        rgot = lax.ppermute(bwd, axis, down)
        excl = combine(got, excl)
        rexcl = combine(rgot, rexcl)
        if 2 * shift < count:
            fwd = combine(got, fwd)
            bwd = combine(rgot, bwd)
        shift *= 2
    return excl, rexcl


def row_exchange(parts, axis, group):
    count = lax.axis_size(axis)
    place = lax.axis_index(axis) % group

    def ring(step):
        return [
            (base + j, base + (j + step) % group)
            for base in range(0, count, group)
            for j in range(group)
        ]

    def piece(step):
        return lax.dynamic_index_in_dim(parts, (place + step) % group, 0, False)

    got = [lax.dynamic_index_in_dim(parts, place, 0, False)]
    if group != 4 or parts.shape[1] % 2:
        got += [lax.ppermute(piece(step), axis, ring(step)) for step in range(1, group)]
    else:
        half = parts.shape[1] // 2
        far = piece(2)
        near = lax.ppermute(far[:half], axis, ring(2))
        first = lax.ppermute(piece(1), axis, ring(1))
        back = lax.ppermute(jnp.concatenate([piece(3), far[half:]], axis=0), axis, ring(3))
        relay = lax.ppermute(back[parts.shape[1] :], axis, ring(3))
        got += [first, jnp.concatenate([near, relay], axis=0), back[: parts.shape[1]]]
    return jnp.stack([lax.select_n((place - j) % group, *got) for j in range(group)])


def carried_both(decay, forward_part, backward_part, axis):
    count = lax.axis_size(axis)
    group = 4 if count % 4 == 0 and forward_part.shape[0] % 4 == 0 else 1
    heads, rows, cols = forward_part.shape
    share = heads // group
    pad = jnp.broadcast_to(decay[:, None, None], (heads, 8, cols))
    parts = jnp.concatenate([forward_part, backward_part, pad], axis=1)
    mine = row_exchange(parts.reshape(group, share, 2 * rows + 8, cols), axis, group)
    own_s = mine[:, :, :rows]
    own_b = mine[:, :, rows : 2 * rows]
    own_a = mine[:, :, 2 * rows, 0]
    excl = [jnp.zeros_like(own_s[0])]
    excl_a = [jnp.ones_like(own_a[0])]
    for j in range(1, group):
        excl.append(own_a[j - 1][:, None, None] * excl[j - 1] + own_s[j - 1])
        excl_a.append(excl_a[j - 1] * own_a[j - 1])
    total = own_a[group - 1][:, None, None] * excl[group - 1] + own_s[group - 1]
    total_a = excl_a[group - 1] * own_a[group - 1]
    later = [None] * group
    later_a = [None] * group
    later[group - 1] = jnp.zeros_like(own_b[0])
    later_a[group - 1] = jnp.ones_like(own_a[0])
    for j in range(group - 2, -1, -1):
        later[j] = own_b[j + 1] + own_a[j + 1][:, None, None] * later[j + 1]
        later_a[j] = own_a[j + 1] * later_a[j + 1]
    rtotal = own_b[0] + own_a[0][:, None, None] * later[0]
    before, after = group_scan(
        packed(total_a, total), packed(total_a, rtotal), axis, group
    )
    before = before[:, :rows]
    after = after[:, :rows]
    result = jnp.stack(
        [
            jnp.concatenate(
                [
                    excl_a[j][:, None, None] * before + excl[j],
                    later[j] + later_a[j][:, None, None] * after,
                ],
                axis=1,
            )
            for j in range(group)
        ]
    )
    full = row_exchange(result, axis, group).reshape(heads, 2 * rows, cols)
    return full[:, :rows], full[:, rows:]


def digit_sum(value, axis, step, radix):
    count = lax.axis_size(axis)
    digit = (lax.axis_index(axis) // step) % radix
    got = [value]
    for k in range(1, radix):
        got.append(lax.ppermute(value, axis, [(i, i ^ (k * step)) for i in range(count)]))
    total = lax.select_n(digit, *got)
    for m in range(1, radix):
        total = total + lax.select_n(digit ^ m, *got)
    return total


def all_sum(value, axes):
    for axis in axes:
        count = lax.axis_size(axis)
        step = 1
        while step < count:
            radix = 4 if count % (step * 4) == 0 else 2
            value = digit_sum(value, axis, step, radix)
            step *= radix
    return value


def block_mask_list(head_decay_rate, cutoff_list, row_position, start_list):
    is_start = jnp.any(row_position[:, None] == start_list[None, :], axis=1)
    seg_local = jnp.cumsum(is_start.astype(jnp.int32))
    begin = jnp.max(
        jnp.where(start_list[None, :] <= row_position[:, None], start_list[None, :], 0), axis=1
    )
    position = (row_position - begin).astype(jnp.float32)
    logarithm_step = (
        cutoff_list.astype(jnp.float32)[:, None] * cutoff_logarithm - head_decay_rate[None, :]
    )
    cum_log = jnp.cumsum(logarithm_step, axis=0)
    carry_in = jnp.where((seg_local == 0)[:, None], jnp.exp(cum_log), 0.0)
    carry_out = jnp.where(
        (seg_local == seg_local[-1])[:, None], jnp.exp(cum_log[-1][None, :] - cum_log), 0.0
    )
    decay_all = jnp.where(seg_local[-1] == 0, jnp.exp(cum_log[-1]), 0.0)
    return (cum_log, seg_local, position, carry_in, carry_out, decay_all)


def weights_of(cum_log, seg_local):
    count = seg_local.shape[0]
    index = jnp.arange(count, dtype=jnp.int32)
    allowed = (seg_local[:, None] == seg_local[None, :]) & (index[:, None] >= index[None, :])
    spread = cum_log.T[:, :, None] - cum_log.T[:, None, :]
    return jnp.where(allowed[None], jnp.exp(jnp.where(allowed[None], spread, 0.0)), 0.0)


def on_device(
    queries, keys, values, output_gradient, document_lengths, cutoff_rows, head_decay_rate
):
    row_count = queries.shape[1]
    query_block = queries.reshape(row_count, HEADS, HEAD_DIM)
    key_block = keys.reshape(row_count, HEADS, HEAD_DIM)
    value_block = values.reshape(row_count, HEADS, HEAD_DIM)
    gradient_block = output_gradient.reshape(row_count, HEADS, HEAD_DIM)
    block_piece = lax.axis_index("seq")
    row_position = block_piece * row_count + jnp.arange(row_count, dtype=jnp.int32)
    length_list = document_lengths[0]
    start_list = jnp.cumsum(length_list) - length_list
    cum_log, seg_local, position, carry_in, carry_out, decay_all = block_mask_list(
        head_decay_rate, cutoff_rows[0], row_position, start_list
    )
    key_f = key_block.astype(jnp.float32)
    value_f = value_block.astype(jnp.float32)
    grad_f = gradient_block.astype(jnp.float32)
    query_f = query_block.astype(jnp.float32)
    state_local = jnp.einsum(
        "the,thf->hef", carry_out[:, :, None] * key_f, value_f, precision=state_mode
    )
    back_local = jnp.einsum(
        "she,shf->hef", carry_in[:, :, None] * query_f, grad_f, precision=state_mode
    )
    state_input, backward_input = carried_both(decay_all, state_local, back_local, "seq")
    weight = weights_of(cum_log, seg_local)
    scores = jnp.einsum("she,the->hst", query_block, key_block, preferred_element_type=jnp.float32)
    grad_scores = jnp.einsum(
        "shf,thf->hst", gradient_block, value_block, preferred_element_type=jnp.float32
    )
    attn_prob = (weight * scores).astype(jnp.bfloat16)
    grad_prob = (weight * grad_scores).astype(jnp.bfloat16)
    value_full = jnp.einsum(
        "hst,shf->thf", attn_prob, gradient_block, preferred_element_type=jnp.float32
    )
    value_full = value_full + carry_out[:, :, None] * jnp.einsum(
        "the,hef->thf", key_f, backward_input, precision=state_mode
    )
    query_full = jnp.einsum(
        "hst,the->she", grad_prob, key_block, preferred_element_type=jnp.float32
    )
    query_full = query_full + carry_in[:, :, None] * jnp.einsum(
        "shf,hef->she", grad_f, state_input, precision=state_mode
    )
    key_full = jnp.einsum(
        "hst,she->the", grad_prob, query_block, preferred_element_type=jnp.float32
    )
    key_full = key_full + carry_out[:, :, None] * jnp.einsum(
        "thf,hef->the", value_f, backward_input, precision=state_mode
    )
    inner_step = jnp.sum(key_f * key_full, axis=2) - jnp.sum(query_f * query_full, axis=2)
    rate_part = jnp.sum(position[:, None] * inner_step, axis=0)
    rate_total = all_sum(rate_part, ("seq", "dp"))
    token_total = row_count * lax.axis_size("seq") * lax.axis_size("dp")
    rate_grad = head_decay_rate * rate_total / math.sqrt(token_total)
    out_shape = (1, row_count, HEADS * HEAD_DIM)
    return (
        query_full.astype(jnp.bfloat16).reshape(out_shape),
        key_full.astype(jnp.bfloat16).reshape(out_shape),
        value_full.astype(jnp.bfloat16).reshape(out_shape),
        rate_grad,
    )


def solution(mesh):
    in_specs = (
        P("dp", "seq", None),
        P("dp", "seq", None),
        P("dp", "seq", None),
        P("dp", "seq", None),
        P("dp", None),
        P("dp", "seq"),
        P(),
    )
    out_specs = (P("dp", "seq", None), P("dp", "seq", None), P("dp", "seq", None), P())
    return jax.shard_map(
        on_device, mesh=mesh, in_specs=in_specs, out_specs=out_specs, check_vma=False
    )
```

```python
import math

import jax
import jax.numpy as jnp
from jax import lax
from jax.sharding import PartitionSpec as P

HEADS = 16
HEAD_DIM = 128


cutoff_logarithm = math.log(0.7)
state_mode = lax.Precision.HIGH


def packed(decay, state):
    pad = jnp.broadcast_to(decay[:, None, None], (state.shape[0], 8, state.shape[2]))
    return jnp.concatenate([state, pad], axis=1)


def combine(far, near):
    rows = far.shape[1] - 8
    state = near[:, rows : rows + 1, 0:1] * far[:, :rows] + near[:, :rows]
    return jnp.concatenate([state, far[:, rows:] * near[:, rows:]], axis=1)


def group_scan(fwd, bwd, axis, stride):
    count = lax.axis_size(axis)
    excl = jnp.concatenate([jnp.zeros_like(fwd[:, :-8]), jnp.ones_like(fwd[:, -8:])], axis=1)
    rexcl = excl
    shift = stride
    while shift < count:
        up = [(i, i + shift) for i in range(count - shift)]
        down = [(i + shift, i) for i in range(count - shift)]
        got = lax.ppermute(fwd, axis, up)
        rgot = lax.ppermute(bwd, axis, down)
        excl = combine(got, excl)
        rexcl = combine(rgot, rexcl)
        if 2 * shift < count:
            fwd = combine(got, fwd)
            bwd = combine(rgot, bwd)
        shift *= 2
    return excl, rexcl


def row_exchange(parts, axis, group):
    count = lax.axis_size(axis)
    place = lax.axis_index(axis) % group
    got = [lax.dynamic_index_in_dim(parts, place, 0, False)]
    for step in range(1, group):
        pairs = [
            (base + j, base + (j + step) % group)
            for base in range(0, count, group)
            for j in range(group)
        ]
        send = lax.dynamic_index_in_dim(parts, (place + step) % group, 0, False)
        got.append(lax.ppermute(send, axis, pairs))
    return jnp.stack([lax.select_n((place - j) % group, *got) for j in range(group)])


def carried_both(decay, forward_part, backward_part, axis):
    count = lax.axis_size(axis)
    group = 4 if count % 4 == 0 and forward_part.shape[0] % 4 == 0 else 1
    heads, rows, cols = forward_part.shape
    share = heads // group
    pad = jnp.broadcast_to(decay[:, None, None], (heads, 8, cols))
    parts = jnp.concatenate([forward_part, backward_part, pad], axis=1)
    mine = row_exchange(parts.reshape(group, share, 2 * rows + 8, cols), axis, group)
    own_s = mine[:, :, :rows]
    own_b = mine[:, :, rows : 2 * rows]
    own_a = mine[:, :, 2 * rows, 0]
    excl = [jnp.zeros_like(own_s[0])]
    excl_a = [jnp.ones_like(own_a[0])]
    for j in range(1, group):
        excl.append(own_a[j - 1][:, None, None] * excl[j - 1] + own_s[j - 1])
        excl_a.append(excl_a[j - 1] * own_a[j - 1])
    total = own_a[group - 1][:, None, None] * excl[group - 1] + own_s[group - 1]
    total_a = excl_a[group - 1] * own_a[group - 1]
    later = [None] * group
    later_a = [None] * group
    later[group - 1] = jnp.zeros_like(own_b[0])
    later_a[group - 1] = jnp.ones_like(own_a[0])
    for j in range(group - 2, -1, -1):
        later[j] = own_b[j + 1] + own_a[j + 1][:, None, None] * later[j + 1]
        later_a[j] = own_a[j + 1] * later_a[j + 1]
    rtotal = own_b[0] + own_a[0][:, None, None] * later[0]
    before, after = group_scan(
        packed(total_a, total), packed(total_a, rtotal), axis, group
    )
    before = before[:, :rows]
    after = after[:, :rows]
    result = jnp.stack(
        [
            jnp.concatenate(
                [
                    excl_a[j][:, None, None] * before + excl[j],
                    later[j] + later_a[j][:, None, None] * after,
                ],
                axis=1,
            )
            for j in range(group)
        ]
    )
    full = row_exchange(result, axis, group).reshape(heads, 2 * rows, cols)
    return full[:, :rows], full[:, rows:]


def digit_sum(value, axis, step, radix):
    count = lax.axis_size(axis)
    digit = (lax.axis_index(axis) // step) % radix
    got = [value]
    for k in range(1, radix):
        got.append(lax.ppermute(value, axis, [(i, i ^ (k * step)) for i in range(count)]))
    total = lax.select_n(digit, *got)
    for m in range(1, radix):
        total = total + lax.select_n(digit ^ m, *got)
    return total


def all_sum(value, axes):
    for axis in axes:
        count = lax.axis_size(axis)
        step = 1
        while step < count:
            radix = 4 if count % (step * 4) == 0 else 2
            value = digit_sum(value, axis, step, radix)
            step *= radix
    return value


def block_mask_list(head_decay_rate, cutoff_list, row_position, start_list):
    is_start = jnp.any(row_position[:, None] == start_list[None, :], axis=1)
    seg_local = jnp.cumsum(is_start.astype(jnp.int32))
    begin = jnp.max(
        jnp.where(start_list[None, :] <= row_position[:, None], start_list[None, :], 0), axis=1
    )
    position = (row_position - begin).astype(jnp.float32)
    logarithm_step = (
        cutoff_list.astype(jnp.float32)[:, None] * cutoff_logarithm - head_decay_rate[None, :]
    )
    cum_log = jnp.cumsum(logarithm_step, axis=0)
    carry_in = jnp.where((seg_local == 0)[:, None], jnp.exp(cum_log), 0.0)
    carry_out = jnp.where(
        (seg_local == seg_local[-1])[:, None], jnp.exp(cum_log[-1][None, :] - cum_log), 0.0
    )
    decay_all = jnp.where(seg_local[-1] == 0, jnp.exp(cum_log[-1]), 0.0)
    return (cum_log, seg_local, position, carry_in, carry_out, decay_all)


def weights_of(cum_log, seg_local):
    count = seg_local.shape[0]
    index = jnp.arange(count, dtype=jnp.int32)
    allowed = (seg_local[:, None] == seg_local[None, :]) & (index[:, None] >= index[None, :])
    spread = cum_log.T[:, :, None] - cum_log.T[:, None, :]
    return jnp.where(allowed[None], jnp.exp(jnp.where(allowed[None], spread, 0.0)), 0.0)


def on_device(
    queries, keys, values, output_gradient, document_lengths, cutoff_rows, head_decay_rate
):
    row_count = queries.shape[1]
    query_block = queries.reshape(row_count, HEADS, HEAD_DIM)
    key_block = keys.reshape(row_count, HEADS, HEAD_DIM)
    value_block = values.reshape(row_count, HEADS, HEAD_DIM)
    gradient_block = output_gradient.reshape(row_count, HEADS, HEAD_DIM)
    block_piece = lax.axis_index("seq")
    row_position = block_piece * row_count + jnp.arange(row_count, dtype=jnp.int32)
    length_list = document_lengths[0]
    start_list = jnp.cumsum(length_list) - length_list
    cum_log, seg_local, position, carry_in, carry_out, decay_all = block_mask_list(
        head_decay_rate, cutoff_rows[0], row_position, start_list
    )
    key_f = key_block.astype(jnp.float32)
    value_f = value_block.astype(jnp.float32)
    grad_f = gradient_block.astype(jnp.float32)
    query_f = query_block.astype(jnp.float32)
    state_local = jnp.einsum(
        "the,thf->hef", carry_out[:, :, None] * key_f, value_f, precision=state_mode
    )
    back_local = jnp.einsum(
        "she,shf->hef", carry_in[:, :, None] * query_f, grad_f, precision=state_mode
    )
    state_input, backward_input = carried_both(decay_all, state_local, back_local, "seq")
    weight = weights_of(cum_log, seg_local)
    scores = jnp.einsum("she,the->hst", query_block, key_block, preferred_element_type=jnp.float32)
    grad_scores = jnp.einsum(
        "shf,thf->hst", gradient_block, value_block, preferred_element_type=jnp.float32
    )
    attn_prob = (weight * scores).astype(jnp.bfloat16)
    grad_prob = (weight * grad_scores).astype(jnp.bfloat16)
    value_full = jnp.einsum(
        "hst,shf->thf", attn_prob, gradient_block, preferred_element_type=jnp.float32
    )
    value_full = value_full + carry_out[:, :, None] * jnp.einsum(
        "the,hef->thf", key_f, backward_input, precision=state_mode
    )
    query_full = jnp.einsum(
        "hst,the->she", grad_prob, key_block, preferred_element_type=jnp.float32
    )
    query_full = query_full + carry_in[:, :, None] * jnp.einsum(
        "shf,hef->she", grad_f, state_input, precision=state_mode
    )
    key_full = jnp.einsum(
        "hst,she->the", grad_prob, query_block, preferred_element_type=jnp.float32
    )
    key_full = key_full + carry_out[:, :, None] * jnp.einsum(
        "thf,hef->the", value_f, backward_input, precision=state_mode
    )
    inner_step = jnp.sum(key_f * key_full, axis=2) - jnp.sum(query_f * query_full, axis=2)
    rate_part = jnp.sum(position[:, None] * inner_step, axis=0)
    rate_total = all_sum(rate_part, ("dp", "seq"))
    token_total = row_count * lax.axis_size("seq") * lax.axis_size("dp")
    rate_grad = head_decay_rate * rate_total / math.sqrt(token_total)
    out_shape = (1, row_count, HEADS * HEAD_DIM)
    return (
        query_full.astype(jnp.bfloat16).reshape(out_shape),
        key_full.astype(jnp.bfloat16).reshape(out_shape),
        value_full.astype(jnp.bfloat16).reshape(out_shape),
        rate_grad,
    )


def solution(mesh):
    in_specs = (
        P("dp", "seq", None),
        P("dp", "seq", None),
        P("dp", "seq", None),
        P("dp", "seq", None),
        P("dp", None),
        P("dp", "seq"),
        P(),
    )
    out_specs = (P("dp", "seq", None), P("dp", "seq", None), P("dp", "seq", None), P())
    return jax.shard_map(
        on_device, mesh=mesh, in_specs=in_specs, out_specs=out_specs, check_vma=False
    )
```

```python
import math

import jax
import jax.numpy as jnp
from jax import lax
from jax.sharding import PartitionSpec as P

HEADS = 16
HEAD_DIM = 128


cutoff_logarithm = math.log(0.7)
state_mode = lax.Precision.HIGH


def packed(decay, state):
    pad = jnp.broadcast_to(decay[:, None, None], (state.shape[0], 8, state.shape[2]))
    return jnp.concatenate([state, pad], axis=1)


def combine(far, near):
    rows = far.shape[1] - 8
    state = near[:, rows : rows + 1, 0:1] * far[:, :rows] + near[:, :rows]
    return jnp.concatenate([state, far[:, rows:] * near[:, rows:]], axis=1)


def group_scan(fwd, bwd, axis, stride):
    count = lax.axis_size(axis)
    excl = jnp.concatenate([jnp.zeros_like(fwd[:, :-8]), jnp.ones_like(fwd[:, -8:])], axis=1)
    rexcl = excl
    shift = stride
    while shift < count:
        up = [(i, i + shift) for i in range(count - shift)]
        down = [(i + shift, i) for i in range(count - shift)]
        got = lax.ppermute(fwd, axis, up)
        rgot = lax.ppermute(bwd, axis, down)
        excl = combine(got, excl)
        rexcl = combine(rgot, rexcl)
        if 2 * shift < count:
            fwd = combine(got, fwd)
            bwd = combine(rgot, bwd)
        shift *= 2
    return excl, rexcl


def row_exchange(parts, axis, group):
    count = lax.axis_size(axis)
    place = lax.axis_index(axis) % group
    got = [lax.dynamic_index_in_dim(parts, place, 0, False)]
    for step in range(1, group):
        pairs = [
            (base + j, base + (j + step) % group)
            for base in range(0, count, group)
            for j in range(group)
        ]
        send = lax.dynamic_index_in_dim(parts, (place + step) % group, 0, False)
        got.append(lax.ppermute(send, axis, pairs))
    return jnp.stack([lax.select_n((place - j) % group, *got) for j in range(group)])


def carried_both(decay, forward_part, backward_part, axis):
    count = lax.axis_size(axis)
    group = 4 if count % 4 == 0 and forward_part.shape[0] % 4 == 0 else 1
    heads, rows, cols = forward_part.shape
    share = heads // group
    pad = jnp.broadcast_to(decay[:, None, None], (heads, 8, cols))
    parts = jnp.concatenate([forward_part, backward_part, pad], axis=1)
    mine = row_exchange(parts.reshape(group, share, 2 * rows + 8, cols), axis, group)
    own_s = mine[:, :, :rows]
    own_b = mine[:, :, rows : 2 * rows]
    own_a = mine[:, :, 2 * rows, 0]
    excl = [jnp.zeros_like(own_s[0])]
    excl_a = [jnp.ones_like(own_a[0])]
    for j in range(1, group):
        excl.append(own_a[j - 1][:, None, None] * excl[j - 1] + own_s[j - 1])
        excl_a.append(excl_a[j - 1] * own_a[j - 1])
    total = own_a[group - 1][:, None, None] * excl[group - 1] + own_s[group - 1]
    total_a = excl_a[group - 1] * own_a[group - 1]
    later = [None] * group
    later_a = [None] * group
    later[group - 1] = jnp.zeros_like(own_b[0])
    later_a[group - 1] = jnp.ones_like(own_a[0])
    for j in range(group - 2, -1, -1):
        later[j] = own_b[j + 1] + own_a[j + 1][:, None, None] * later[j + 1]
        later_a[j] = own_a[j + 1] * later_a[j + 1]
    rtotal = own_b[0] + own_a[0][:, None, None] * later[0]
    before, after = group_scan(
        packed(total_a, total), packed(total_a, rtotal), axis, group
    )
    before = before[:, :rows]
    after = after[:, :rows]
    result = jnp.stack(
        [
            jnp.concatenate(
                [
                    excl_a[j][:, None, None] * before + excl[j],
                    later[j] + later_a[j][:, None, None] * after,
                ],
                axis=1,
            )
            for j in range(group)
        ]
    )
    full = row_exchange(result, axis, group).reshape(heads, 2 * rows, cols)
    return full[:, :rows], full[:, rows:]


def digit_sum(value, axis, step, radix):
    count = lax.axis_size(axis)
    digit = (lax.axis_index(axis) // step) % radix
    got = [value]
    for k in range(1, radix):
        got.append(lax.ppermute(value, axis, [(i, i ^ (k * step)) for i in range(count)]))
    total = lax.select_n(digit, *got)
    for m in range(1, radix):
        total = total + lax.select_n(digit ^ m, *got)
    return total


def all_sum(value, axes):
    for axis in axes:
        count = lax.axis_size(axis)
        step = 1
        while step < count:
            radix = count if count <= 8 else (4 if count % (step * 4) == 0 else 2)
            value = digit_sum(value, axis, step, radix)
            step *= radix
    return value


def block_mask_list(head_decay_rate, cutoff_list, row_position, start_list):
    is_start = jnp.any(row_position[:, None] == start_list[None, :], axis=1)
    seg_local = jnp.cumsum(is_start.astype(jnp.int32))
    begin = jnp.max(
        jnp.where(start_list[None, :] <= row_position[:, None], start_list[None, :], 0), axis=1
    )
    position = (row_position - begin).astype(jnp.float32)
    logarithm_step = (
        cutoff_list.astype(jnp.float32)[:, None] * cutoff_logarithm - head_decay_rate[None, :]
    )
    cum_log = jnp.cumsum(logarithm_step, axis=0)
    carry_in = jnp.where((seg_local == 0)[:, None], jnp.exp(cum_log), 0.0)
    carry_out = jnp.where(
        (seg_local == seg_local[-1])[:, None], jnp.exp(cum_log[-1][None, :] - cum_log), 0.0
    )
    decay_all = jnp.where(seg_local[-1] == 0, jnp.exp(cum_log[-1]), 0.0)
    return (cum_log, seg_local, position, carry_in, carry_out, decay_all)


def weights_of(cum_log, seg_local):
    count = seg_local.shape[0]
    index = jnp.arange(count, dtype=jnp.int32)
    allowed = (seg_local[:, None] == seg_local[None, :]) & (index[:, None] >= index[None, :])
    spread = cum_log.T[:, :, None] - cum_log.T[:, None, :]
    return jnp.where(allowed[None], jnp.exp(jnp.where(allowed[None], spread, 0.0)), 0.0)


def on_device(
    queries, keys, values, output_gradient, document_lengths, cutoff_rows, head_decay_rate
):
    row_count = queries.shape[1]
    query_block = queries.reshape(row_count, HEADS, HEAD_DIM)
    key_block = keys.reshape(row_count, HEADS, HEAD_DIM)
    value_block = values.reshape(row_count, HEADS, HEAD_DIM)
    gradient_block = output_gradient.reshape(row_count, HEADS, HEAD_DIM)
    block_piece = lax.axis_index("seq")
    row_position = block_piece * row_count + jnp.arange(row_count, dtype=jnp.int32)
    length_list = document_lengths[0]
    start_list = jnp.cumsum(length_list) - length_list
    cum_log, seg_local, position, carry_in, carry_out, decay_all = block_mask_list(
        head_decay_rate, cutoff_rows[0], row_position, start_list
    )
    key_f = key_block.astype(jnp.float32)
    value_f = value_block.astype(jnp.float32)
    grad_f = gradient_block.astype(jnp.float32)
    query_f = query_block.astype(jnp.float32)
    state_local = jnp.einsum(
        "the,thf->hef", carry_out[:, :, None] * key_f, value_f, precision=state_mode
    )
    back_local = jnp.einsum(
        "she,shf->hef", carry_in[:, :, None] * query_f, grad_f, precision=state_mode
    )
    state_input, backward_input = carried_both(decay_all, state_local, back_local, "seq")
    weight = weights_of(cum_log, seg_local)
    scores = jnp.einsum("she,the->hst", query_block, key_block, preferred_element_type=jnp.float32)
    grad_scores = jnp.einsum(
        "shf,thf->hst", gradient_block, value_block, preferred_element_type=jnp.float32
    )
    attn_prob = (weight * scores).astype(jnp.bfloat16)
    grad_prob = (weight * grad_scores).astype(jnp.bfloat16)
    value_full = jnp.einsum(
        "hst,shf->thf", attn_prob, gradient_block, preferred_element_type=jnp.float32
    )
    value_full = value_full + carry_out[:, :, None] * jnp.einsum(
        "the,hef->thf", key_f, backward_input, precision=state_mode
    )
    query_full = jnp.einsum(
        "hst,the->she", grad_prob, key_block, preferred_element_type=jnp.float32
    )
    query_full = query_full + carry_in[:, :, None] * jnp.einsum(
        "shf,hef->she", grad_f, state_input, precision=state_mode
    )
    key_full = jnp.einsum(
        "hst,she->the", grad_prob, query_block, preferred_element_type=jnp.float32
    )
    key_full = key_full + carry_out[:, :, None] * jnp.einsum(
        "thf,hef->the", value_f, backward_input, precision=state_mode
    )
    inner_step = jnp.sum(key_f * key_full, axis=2) - jnp.sum(query_f * query_full, axis=2)
    rate_part = jnp.sum(position[:, None] * inner_step, axis=0)
    rate_total = all_sum(rate_part, ("seq", "dp"))
    token_total = row_count * lax.axis_size("seq") * lax.axis_size("dp")
    rate_grad = head_decay_rate * rate_total / math.sqrt(token_total)
    out_shape = (1, row_count, HEADS * HEAD_DIM)
    return (
        query_full.astype(jnp.bfloat16).reshape(out_shape),
        key_full.astype(jnp.bfloat16).reshape(out_shape),
        value_full.astype(jnp.bfloat16).reshape(out_shape),
        rate_grad,
    )


def solution(mesh):
    in_specs = (
        P("dp", "seq", None),
        P("dp", "seq", None),
        P("dp", "seq", None),
        P("dp", "seq", None),
        P("dp", None),
        P("dp", "seq"),
        P(),
    )
    out_specs = (P("dp", "seq", None), P("dp", "seq", None), P("dp", "seq", None), P())
    return jax.shard_map(
        on_device, mesh=mesh, in_specs=in_specs, out_specs=out_specs, check_vma=False
    )
```

```python
import math

import jax
import jax.numpy as jnp
from jax import lax
from jax.sharding import PartitionSpec as P

HEADS = 16
HEAD_DIM = 128


cutoff_logarithm = math.log(0.7)
state_mode = lax.Precision.HIGH


def packed(decay, state):
    pad = jnp.broadcast_to(decay[:, None, None], (state.shape[0], 8, state.shape[2]))
    return jnp.concatenate([state, pad], axis=1)


def combine(far, near):
    rows = far.shape[1] - 8
    state = near[:, rows : rows + 1, 0:1] * far[:, :rows] + near[:, :rows]
    return jnp.concatenate([state, far[:, rows:] * near[:, rows:]], axis=1)


def group_scan(fwd, bwd, axis, stride):
    count = lax.axis_size(axis)
    excl = jnp.concatenate([jnp.zeros_like(fwd[:, :-8]), jnp.ones_like(fwd[:, -8:])], axis=1)
    rexcl = excl
    shift = stride
    while shift < count:
        up = [(i, i + shift) for i in range(count - shift)]
        down = [(i + shift, i) for i in range(count - shift)]
        got = lax.ppermute(fwd, axis, up)
        rgot = lax.ppermute(bwd, axis, down)
        excl = combine(got, excl)
        rexcl = combine(rgot, rexcl)
        if 2 * shift < count:
            fwd = combine(got, fwd)
            bwd = combine(rgot, bwd)
        shift *= 2
    return excl, rexcl


def row_exchange(parts, axis, group):
    count = lax.axis_size(axis)
    place = lax.axis_index(axis) % group
    got = [lax.dynamic_index_in_dim(parts, place, 0, False)]
    for step in range(1, group):
        pairs = [
            (base + j, base + (j + step) % group)
            for base in range(0, count, group)
            for j in range(group)
        ]
        send = lax.dynamic_index_in_dim(parts, (place + step) % group, 0, False)
        got.append(lax.ppermute(send, axis, pairs))
    return jnp.stack([lax.select_n((place - j) % group, *got) for j in range(group)])


def carried_both(decay, forward_part, backward_part, axis):
    count = lax.axis_size(axis)
    group = 4 if count % 4 == 0 and forward_part.shape[0] % 4 == 0 else 1
    heads, rows, cols = forward_part.shape
    share = heads // group
    pad = jnp.broadcast_to(decay[:, None, None], (heads, 8, cols))
    parts = jnp.concatenate([forward_part, backward_part, pad], axis=1)
    mine = row_exchange(parts.reshape(group, share, 2 * rows + 8, cols), axis, group)
    own_s = mine[:, :, :rows]
    own_b = mine[:, :, rows : 2 * rows]
    own_a = mine[:, :, 2 * rows, 0]
    excl = [jnp.zeros_like(own_s[0])]
    excl_a = [jnp.ones_like(own_a[0])]
    for j in range(1, group):
        excl.append(own_a[j - 1][:, None, None] * excl[j - 1] + own_s[j - 1])
        excl_a.append(excl_a[j - 1] * own_a[j - 1])
    total = own_s[group - 1]
    for j in range(group - 1):
        scale = own_a[j + 1]
        for k in range(j + 2, group):
            scale = scale * own_a[k]
        total = total + scale[:, None, None] * own_s[j]
    total_a = excl_a[group - 1] * own_a[group - 1]
    later = [None] * group
    later_a = [None] * group
    later[group - 1] = jnp.zeros_like(own_b[0])
    later_a[group - 1] = jnp.ones_like(own_a[0])
    for j in range(group - 2, -1, -1):
        later[j] = own_b[j + 1] + own_a[j + 1][:, None, None] * later[j + 1]
        later_a[j] = own_a[j + 1] * later_a[j + 1]
    rtotal = own_b[0]
    for j in range(1, group):
        scale = own_a[0]
        for k in range(1, j):
            scale = scale * own_a[k]
        rtotal = rtotal + scale[:, None, None] * own_b[j]
    before, after = group_scan(
        packed(total_a, total), packed(total_a, rtotal), axis, group
    )
    before = before[:, :rows]
    after = after[:, :rows]
    result = jnp.stack(
        [
            jnp.concatenate(
                [
                    excl_a[j][:, None, None] * before + excl[j],
                    later[j] + later_a[j][:, None, None] * after,
                ],
                axis=1,
            )
            for j in range(group)
        ]
    )
    full = row_exchange(result, axis, group).reshape(heads, 2 * rows, cols)
    return full[:, :rows], full[:, rows:]


def digit_sum(value, axis, step, radix):
    count = lax.axis_size(axis)
    digit = (lax.axis_index(axis) // step) % radix
    got = [value]
    for k in range(1, radix):
        got.append(lax.ppermute(value, axis, [(i, i ^ (k * step)) for i in range(count)]))
    total = lax.select_n(digit, *got)
    for m in range(1, radix):
        total = total + lax.select_n(digit ^ m, *got)
    return total


def all_sum(value, axes):
    for axis in axes:
        count = lax.axis_size(axis)
        step = 1
        while step < count:
            radix = 4 if count % (step * 4) == 0 else 2
            value = digit_sum(value, axis, step, radix)
            step *= radix
    return value


def block_mask_list(head_decay_rate, cutoff_list, row_position, start_list):
    is_start = jnp.any(row_position[:, None] == start_list[None, :], axis=1)
    seg_local = jnp.cumsum(is_start.astype(jnp.int32))
    begin = jnp.max(
        jnp.where(start_list[None, :] <= row_position[:, None], start_list[None, :], 0), axis=1
    )
    position = (row_position - begin).astype(jnp.float32)
    logarithm_step = (
        cutoff_list.astype(jnp.float32)[:, None] * cutoff_logarithm - head_decay_rate[None, :]
    )
    cum_log = jnp.cumsum(logarithm_step, axis=0)
    carry_in = jnp.where((seg_local == 0)[:, None], jnp.exp(cum_log), 0.0)
    carry_out = jnp.where(
        (seg_local == seg_local[-1])[:, None], jnp.exp(cum_log[-1][None, :] - cum_log), 0.0
    )
    decay_all = jnp.where(seg_local[-1] == 0, jnp.exp(cum_log[-1]), 0.0)
    return (cum_log, seg_local, position, carry_in, carry_out, decay_all)


def weights_of(cum_log, seg_local):
    count = seg_local.shape[0]
    index = jnp.arange(count, dtype=jnp.int32)
    allowed = (seg_local[:, None] == seg_local[None, :]) & (index[:, None] >= index[None, :])
    spread = cum_log.T[:, :, None] - cum_log.T[:, None, :]
    return jnp.where(allowed[None], jnp.exp(jnp.where(allowed[None], spread, 0.0)), 0.0)


def on_device(
    queries, keys, values, output_gradient, document_lengths, cutoff_rows, head_decay_rate
):
    row_count = queries.shape[1]
    query_block = queries.reshape(row_count, HEADS, HEAD_DIM)
    key_block = keys.reshape(row_count, HEADS, HEAD_DIM)
    value_block = values.reshape(row_count, HEADS, HEAD_DIM)
    gradient_block = output_gradient.reshape(row_count, HEADS, HEAD_DIM)
    block_piece = lax.axis_index("seq")
    row_position = block_piece * row_count + jnp.arange(row_count, dtype=jnp.int32)
    length_list = document_lengths[0]
    start_list = jnp.cumsum(length_list) - length_list
    cum_log, seg_local, position, carry_in, carry_out, decay_all = block_mask_list(
        head_decay_rate, cutoff_rows[0], row_position, start_list
    )
    key_f = key_block.astype(jnp.float32)
    value_f = value_block.astype(jnp.float32)
    grad_f = gradient_block.astype(jnp.float32)
    query_f = query_block.astype(jnp.float32)
    state_local = jnp.einsum(
        "the,thf->hef", carry_out[:, :, None] * key_f, value_f, precision=state_mode
    )
    back_local = jnp.einsum(
        "she,shf->hef", carry_in[:, :, None] * query_f, grad_f, precision=state_mode
    )
    state_input, backward_input = carried_both(decay_all, state_local, back_local, "seq")
    weight = weights_of(cum_log, seg_local)
    scores = jnp.einsum("she,the->hst", query_block, key_block, preferred_element_type=jnp.float32)
    grad_scores = jnp.einsum(
        "shf,thf->hst", gradient_block, value_block, preferred_element_type=jnp.float32
    )
    attn_prob = (weight * scores).astype(jnp.bfloat16)
    grad_prob = (weight * grad_scores).astype(jnp.bfloat16)
    value_full = jnp.einsum(
        "hst,shf->thf", attn_prob, gradient_block, preferred_element_type=jnp.float32
    )
    value_full = value_full + carry_out[:, :, None] * jnp.einsum(
        "the,hef->thf", key_f, backward_input, precision=state_mode
    )
    query_full = jnp.einsum(
        "hst,the->she", grad_prob, key_block, preferred_element_type=jnp.float32
    )
    query_full = query_full + carry_in[:, :, None] * jnp.einsum(
        "shf,hef->she", grad_f, state_input, precision=state_mode
    )
    key_full = jnp.einsum(
        "hst,she->the", grad_prob, query_block, preferred_element_type=jnp.float32
    )
    key_full = key_full + carry_out[:, :, None] * jnp.einsum(
        "thf,hef->the", value_f, backward_input, precision=state_mode
    )
    inner_step = jnp.sum(key_f * key_full, axis=2) - jnp.sum(query_f * query_full, axis=2)
    rate_part = jnp.sum(position[:, None] * inner_step, axis=0)
    rate_total = all_sum(rate_part, ("seq", "dp"))
    token_total = row_count * lax.axis_size("seq") * lax.axis_size("dp")
    rate_grad = head_decay_rate * rate_total / math.sqrt(token_total)
    out_shape = (1, row_count, HEADS * HEAD_DIM)
    return (
        query_full.astype(jnp.bfloat16).reshape(out_shape),
        key_full.astype(jnp.bfloat16).reshape(out_shape),
        value_full.astype(jnp.bfloat16).reshape(out_shape),
        rate_grad,
    )


def solution(mesh):
    in_specs = (
        P("dp", "seq", None),
        P("dp", "seq", None),
        P("dp", "seq", None),
        P("dp", "seq", None),
        P("dp", None),
        P("dp", "seq"),
        P(),
    )
    out_specs = (P("dp", "seq", None), P("dp", "seq", None), P("dp", "seq", None), P())
    return jax.shard_map(
        on_device, mesh=mesh, in_specs=in_specs, out_specs=out_specs, check_vma=False
    )
```

```python
import math

import jax
import jax.numpy as jnp
from jax import lax
from jax.sharding import PartitionSpec as P

HEADS = 16
HEAD_DIM = 128


cutoff_logarithm = math.log(0.7)
state_mode = lax.Precision.HIGH


def packed(decay, state):
    pad = jnp.broadcast_to(decay[:, None, None], (state.shape[0], 8, state.shape[2]))
    return jnp.concatenate([state, pad], axis=1)


def combine(far, near):
    rows = far.shape[1] - 8
    state = near[:, rows : rows + 1, 0:1] * far[:, :rows] + near[:, :rows]
    return jnp.concatenate([state, far[:, rows:] * near[:, rows:]], axis=1)


def group_scan(fwd, bwd, axis, stride):
    count = lax.axis_size(axis)
    excl = jnp.concatenate([jnp.zeros_like(fwd[:, :-8]), jnp.ones_like(fwd[:, -8:])], axis=1)
    rexcl = excl
    shift = stride
    while shift < count:
        up = [(i, i + shift) for i in range(count - shift)]
        down = [(i + shift, i) for i in range(count - shift)]
        got = lax.ppermute(fwd, axis, up)
        rgot = lax.ppermute(bwd, axis, down)
        excl = combine(got, excl)
        rexcl = combine(rgot, rexcl)
        if 2 * shift < count:
            fwd = combine(got, fwd)
            bwd = combine(rgot, bwd)
        shift *= 2
    return excl, rexcl


def row_exchange(parts, axis, group):
    count = lax.axis_size(axis)
    place = lax.axis_index(axis) % group
    got = [lax.dynamic_index_in_dim(parts, place, 0, False)]
    for step in range(1, group):
        pairs = [
            (base + j, base + (j + step) % group)
            for base in range(0, count, group)
            for j in range(group)
        ]
        send = lax.dynamic_index_in_dim(parts, (place + step) % group, 0, False)
        got.append(lax.ppermute(send, axis, pairs))
    return jnp.stack([lax.select_n((place - j) % group, *got) for j in range(group)])


def carried_both(decay, forward_part, backward_part, axis):
    count = lax.axis_size(axis)
    group = 4 if count % 4 == 0 and forward_part.shape[0] % 4 == 0 else 1
    heads, rows, cols = forward_part.shape
    share = heads // group
    pad = jnp.broadcast_to(decay[:, None, None], (heads, 8, cols))
    parts = jnp.concatenate([forward_part, backward_part, pad], axis=1)
    mine = row_exchange(parts.reshape(group, share, 2 * rows + 8, cols), axis, group)
    own_s = mine[:, :, :rows]
    own_b = mine[:, :, rows : 2 * rows]
    own_a = mine[:, :, 2 * rows, 0]
    excl = [jnp.zeros_like(own_s[0])]
    excl_a = [jnp.ones_like(own_a[0])]
    for j in range(1, group):
        acc = own_s[j - 1]
        for i in range(j - 1):
            scale = own_a[i + 1]
            for k in range(i + 2, j):
                scale = scale * own_a[k]
            acc = acc + scale[:, None, None] * own_s[i]
        excl.append(acc)
        excl_a.append(excl_a[j - 1] * own_a[j - 1])
    total = own_s[group - 1]
    for j in range(group - 1):
        scale = own_a[j + 1]
        for k in range(j + 2, group):
            scale = scale * own_a[k]
        total = total + scale[:, None, None] * own_s[j]
    total_a = excl_a[group - 1] * own_a[group - 1]
    later = [None] * group
    later_a = [None] * group
    later[group - 1] = jnp.zeros_like(own_b[0])
    later_a[group - 1] = jnp.ones_like(own_a[0])
    for j in range(group - 2, -1, -1):
        later[j] = own_b[j + 1] + own_a[j + 1][:, None, None] * later[j + 1]
        later_a[j] = own_a[j + 1] * later_a[j + 1]
    rtotal = own_b[0]
    for j in range(1, group):
        scale = own_a[0]
        for k in range(1, j):
            scale = scale * own_a[k]
        rtotal = rtotal + scale[:, None, None] * own_b[j]
    before, after = group_scan(
        packed(total_a, total), packed(total_a, rtotal), axis, group
    )
    before = before[:, :rows]
    after = after[:, :rows]
    result = jnp.stack(
        [
            jnp.concatenate(
                [
                    excl_a[j][:, None, None] * before + excl[j],
                    later[j] + later_a[j][:, None, None] * after,
                ],
                axis=1,
            )
            for j in range(group)
        ]
    )
    full = row_exchange(result, axis, group).reshape(heads, 2 * rows, cols)
    return full[:, :rows], full[:, rows:]


def digit_sum(value, axis, step, radix):
    count = lax.axis_size(axis)
    digit = (lax.axis_index(axis) // step) % radix
    got = [value]
    for k in range(1, radix):
        got.append(lax.ppermute(value, axis, [(i, i ^ (k * step)) for i in range(count)]))
    total = lax.select_n(digit, *got)
    for m in range(1, radix):
        total = total + lax.select_n(digit ^ m, *got)
    return total


def all_sum(value, axes):
    for axis in axes:
        count = lax.axis_size(axis)
        step = 1
        while step < count:
            radix = 4 if count % (step * 4) == 0 else 2
            value = digit_sum(value, axis, step, radix)
            step *= radix
    return value


def block_mask_list(head_decay_rate, cutoff_list, row_position, start_list):
    is_start = jnp.any(row_position[:, None] == start_list[None, :], axis=1)
    seg_local = jnp.cumsum(is_start.astype(jnp.int32))
    begin = jnp.max(
        jnp.where(start_list[None, :] <= row_position[:, None], start_list[None, :], 0), axis=1
    )
    position = (row_position - begin).astype(jnp.float32)
    logarithm_step = (
        cutoff_list.astype(jnp.float32)[:, None] * cutoff_logarithm - head_decay_rate[None, :]
    )
    cum_log = jnp.cumsum(logarithm_step, axis=0)
    carry_in = jnp.where((seg_local == 0)[:, None], jnp.exp(cum_log), 0.0)
    carry_out = jnp.where(
        (seg_local == seg_local[-1])[:, None], jnp.exp(cum_log[-1][None, :] - cum_log), 0.0
    )
    decay_all = jnp.where(seg_local[-1] == 0, jnp.exp(cum_log[-1]), 0.0)
    return (cum_log, seg_local, position, carry_in, carry_out, decay_all)


def weights_of(cum_log, seg_local):
    count = seg_local.shape[0]
    index = jnp.arange(count, dtype=jnp.int32)
    allowed = (seg_local[:, None] == seg_local[None, :]) & (index[:, None] >= index[None, :])
    spread = cum_log.T[:, :, None] - cum_log.T[:, None, :]
    return jnp.where(allowed[None], jnp.exp(jnp.where(allowed[None], spread, 0.0)), 0.0)


def on_device(
    queries, keys, values, output_gradient, document_lengths, cutoff_rows, head_decay_rate
):
    row_count = queries.shape[1]
    query_block = queries.reshape(row_count, HEADS, HEAD_DIM)
    key_block = keys.reshape(row_count, HEADS, HEAD_DIM)
    value_block = values.reshape(row_count, HEADS, HEAD_DIM)
    gradient_block = output_gradient.reshape(row_count, HEADS, HEAD_DIM)
    block_piece = lax.axis_index("seq")
    row_position = block_piece * row_count + jnp.arange(row_count, dtype=jnp.int32)
    length_list = document_lengths[0]
    start_list = jnp.cumsum(length_list) - length_list
    cum_log, seg_local, position, carry_in, carry_out, decay_all = block_mask_list(
        head_decay_rate, cutoff_rows[0], row_position, start_list
    )
    key_f = key_block.astype(jnp.float32)
    value_f = value_block.astype(jnp.float32)
    grad_f = gradient_block.astype(jnp.float32)
    query_f = query_block.astype(jnp.float32)
    state_local = jnp.einsum(
        "the,thf->hef", carry_out[:, :, None] * key_f, value_f, precision=state_mode
    )
    back_local = jnp.einsum(
        "she,shf->hef", carry_in[:, :, None] * query_f, grad_f, precision=state_mode
    )
    state_input, backward_input = carried_both(decay_all, state_local, back_local, "seq")
    weight = weights_of(cum_log, seg_local)
    scores = jnp.einsum("she,the->hst", query_block, key_block, preferred_element_type=jnp.float32)
    grad_scores = jnp.einsum(
        "shf,thf->hst", gradient_block, value_block, preferred_element_type=jnp.float32
    )
    attn_prob = (weight * scores).astype(jnp.bfloat16)
    grad_prob = (weight * grad_scores).astype(jnp.bfloat16)
    value_full = jnp.einsum(
        "hst,shf->thf", attn_prob, gradient_block, preferred_element_type=jnp.float32
    )
    value_full = value_full + carry_out[:, :, None] * jnp.einsum(
        "the,hef->thf", key_f, backward_input, precision=state_mode
    )
    query_full = jnp.einsum(
        "hst,the->she", grad_prob, key_block, preferred_element_type=jnp.float32
    )
    query_full = query_full + carry_in[:, :, None] * jnp.einsum(
        "shf,hef->she", grad_f, state_input, precision=state_mode
    )
    key_full = jnp.einsum(
        "hst,she->the", grad_prob, query_block, preferred_element_type=jnp.float32
    )
    key_full = key_full + carry_out[:, :, None] * jnp.einsum(
        "thf,hef->the", value_f, backward_input, precision=state_mode
    )
    inner_step = jnp.sum(key_f * key_full, axis=2) - jnp.sum(query_f * query_full, axis=2)
    rate_part = jnp.sum(position[:, None] * inner_step, axis=0)
    rate_total = all_sum(rate_part, ("seq", "dp"))
    token_total = row_count * lax.axis_size("seq") * lax.axis_size("dp")
    rate_grad = head_decay_rate * rate_total / math.sqrt(token_total)
    out_shape = (1, row_count, HEADS * HEAD_DIM)
    return (
        query_full.astype(jnp.bfloat16).reshape(out_shape),
        key_full.astype(jnp.bfloat16).reshape(out_shape),
        value_full.astype(jnp.bfloat16).reshape(out_shape),
        rate_grad,
    )


def solution(mesh):
    in_specs = (
        P("dp", "seq", None),
        P("dp", "seq", None),
        P("dp", "seq", None),
        P("dp", "seq", None),
        P("dp", None),
        P("dp", "seq"),
        P(),
    )
    out_specs = (P("dp", "seq", None), P("dp", "seq", None), P("dp", "seq", None), P())
    return jax.shard_map(
        on_device, mesh=mesh, in_specs=in_specs, out_specs=out_specs, check_vma=False
    )
```
